32 devices in a mesh: groups: 2 (over x), ctx: 16 (over z, y, core).
Axes of the slice: x: 2, y: 2, z: 4, core: 2. Of those that a mesh axis runs over, the one named last changes fastest.
Arguments:
- queries: bfloat16 [8192, 4096], P(('groups', 'ctx')), parts along dimension 0, may hold values from -24 to 24
- key_rows: bfloat16 [8192, 1024], P(('groups', 'ctx')), parts along dimension 0, may hold values from -6 to 6
- value_rows: bfloat16 [8192, 1024], P(('groups', 'ctx')), parts along dimension 0, may hold values from -6 to 6
- pattern: int32 [32, 11], replicated, may hold values from 0 to 31, as said below
Outputs:
- attended: bfloat16 [8192, 4096], P(('groups', 'ctx')), parts along dimension 0
The draws below stay inside these ranges and needn't reach their ends.
There are 2 independent parts, one for each index of `groups`. The reference program is written for one: setup_inputs(seed, part) draws one part's arguments, and reference() takes and returns one part's arrays. A program takes and returns all parts, laid end to end along the dimension named above; an argument that names none is the same for every part. Nothing has to cross between parts.
Inputs may be any that keep to these rules, and one draw needn't show every extreme that they name: `pattern`: entry j < 8 of block b's list is max(b - j, 0); the other 3 entries are multiples of 32 no larger than b, the first of them exactly (b // 32) * 32.
All inputs are finite; a program needn't handle non-finite values.
Results may differ from the reference program's by a relative error of at most 0.0036.
Values may be sent and summed in bfloat16 or wider, within the bound.
No kernel may reach another device: no remote copies, remote signals or barrier semaphores. Data moves between devices by JAX's collectives and lax.ppermute only.
A program may use at most 128 MiB of HBM per device.

```python
import jax
import jax.numpy as jnp
from jax import lax

H = 32
KVH = 8
HD = 128
BLK = 128
WIN = 8
NSTR = 3
STRIDE = 32
LIST = 11
TOKENS = 4096
NBLK = 32


def make_pair(key):
    key_query, key_keys = jax.random.split(jax.random.fold_in(key, 7), 2)
    keys_arr = jax.random.truncated_normal(key_keys, -6.0, 6.0, (TOKENS, KVH * HD), jnp.float32)
    query_arr = 2.0 * jax.random.truncated_normal(key_query, -6.0, 6.0, (TOKENS, H * HD), jnp.float32)
    return (query_arr, keys_arr)


def draw_queries(key, part):
    return make_pair(key)[0].astype(jnp.bfloat16)


def draw_key_rows(key, part):
    return make_pair(key)[1].astype(jnp.bfloat16)


def draw_pattern(key, part):
    blocks_col = jnp.arange(NBLK, dtype=jnp.int32)[:, None]
    lag_steps = jnp.arange(WIN, dtype=jnp.int32)[None, :]
    window = jnp.maximum(blocks_col - lag_steps, 0)
    random_ints = jax.random.randint(jax.random.fold_in(key, 11), (NBLK, NSTR - 1), 0, 1 << 20, jnp.int32)
    column_count = blocks_col // STRIDE + 1
    latest = blocks_col // STRIDE * STRIDE
    stride_cols = random_ints % column_count * STRIDE
    return jnp.concatenate([window, latest, stride_cols], axis=1).astype(jnp.int32)


def level_of(own_key, dims, pieces, low, largest):
    def one(dim, parts):
        steps = jax.random.uniform(jax.random.fold_in(jax.random.fold_in(own_key, 6), dim), (parts,), jnp.float32, low / len(pieces), largest / len(pieces))
        return jnp.repeat(jnp.exp(steps), dims[dim] // parts).reshape((-1,) + (1,) * (len(dims) - dim - 1))

    level = one(*pieces[0])
    for cut in pieces[1:]:
        level = level * one(*cut)
    return level


def normal_values(own_key, dims, spread, reach, pieces=(), held_as=jnp.bfloat16):
    level = level_of(own_key, dims, pieces, -0.22, 0.18) if pieces else 1.0
    values = jax.random.normal(own_key, dims, jnp.float32) * spread * level
    return jnp.minimum(jnp.maximum(values, -reach), reach).astype(held_as)


def setup_inputs(seed: int = 0, part: int = 0) -> dict:
    key_list = jax.random.split(jax.random.key(seed), 5)
    part_splits = jax.random.split(jax.random.fold_in(key_list[4], part), 5)
    return {
        "queries": draw_queries(jax.random.fold_in(jax.random.fold_in(key_list[4], part), 71), part),
        "key_rows": draw_key_rows(jax.random.fold_in(jax.random.fold_in(key_list[4], part), 71), part),
        "value_rows": normal_values(part_splits[2], (TOKENS, KVH * HD), 1.0, 6.0, ((0, 16),)),
        "pattern": draw_pattern(jax.random.fold_in(key_list[4], 71), part),
    }


def attend_block(query_block, key_block, value_block, entries, block):
    group_size = H // KVH
    query = query_block.reshape(BLK, KVH, group_size, HD).astype(jnp.float32)
    keys_f = key_block.reshape(LIST * BLK, KVH, HD).astype(jnp.float32)
    values_f = value_block.reshape(LIST * BLK, KVH, HD).astype(jnp.float32)
    scores = jnp.einsum("qkgd,skd->kgqs", query, keys_f) * (HD ** -0.5)
    query_pos = jnp.arange(BLK, dtype=jnp.int32)
    key_pos = jnp.tile(jnp.arange(BLK, dtype=jnp.int32), LIST)
    on_diagonal = jnp.repeat(entries == block, BLK)
    allowed = jnp.logical_not(on_diagonal)[None, :] | (key_pos[None, :] <= query_pos[:, None])
    scores = jnp.where(allowed[None, None], scores, -jnp.inf)
    row_max = jnp.max(scores, axis=-1, keepdims=True)
    powers = jnp.exp(scores - row_max)
    denominator = jnp.sum(powers, axis=-1)
    weights_bf = powers.astype(jnp.bfloat16)
    weighted = jnp.einsum("kgqs,skd->qkgd", weights_bf.astype(jnp.float32), values_f)
    result = weighted / jnp.transpose(denominator, (2, 0, 1))[..., None]
    return result.astype(jnp.bfloat16).reshape(BLK, H * HD)


def reference(queries, key_rows, value_rows, pattern):
    key_blocks = key_rows.reshape(NBLK, BLK, KVH * HD)
    value_blocks = value_rows.reshape(NBLK, BLK, KVH * HD)

    def per_block(block):
        entries = pattern[block]
        query_block = lax.dynamic_slice_in_dim(queries, (block * BLK).astype(jnp.int32), BLK, 0)
        key_block = key_blocks[entries].reshape(LIST * BLK, KVH * HD)
        value_block = value_blocks[entries].reshape(LIST * BLK, KVH * HD)
        return attend_block(query_block, key_block, value_block, entries, block)

    outputs = lax.map(per_block, jnp.arange(NBLK, dtype=jnp.int32))
    return outputs.reshape(TOKENS, H * HD)
```

```python
import functools

import jax
import jax.numpy as jnp
from jax import lax
from jax.experimental import pallas as pl
from jax.experimental.pallas import tpu as pltpu
from jax.sharding import PartitionSpec as P

H = 32
KVH = 8
HD = 128
BLK = 128
WIN = 8
STRIDE = 32
LIST = 11
GROUP = H // KVH


def passed_along(shard, axis, by):
    size = lax.axis_size(axis)
    pairs = [(i, i + by) for i in range(size) if 0 <= i + by < size]
    return lax.ppermute(shard, axis, pairs)


def tree_broadcast(block, axis, source, size):
    index = lax.axis_index(axis)
    span = size - source
    held = block
    dist = 1
    while dist < span:
        dist *= 2
    dist //= 2
    while dist >= 1:
        pairs = [
            (source + j, source + j + dist)
            for j in range(0, span, 2 * dist)
            if j + dist < span
        ]
        got = lax.ppermute(held, axis, pairs)
        rel = index - source
        takes = (rel >= 0) & (rel % (2 * dist) == dist)
        held = jnp.where(takes, got, held)
        dist //= 2
    return held


def attend_kernel(slot_ref, diag_ref, q_ref, k_ref, v_ref, o_ref, score_sc):
    local = pl.program_id(1)
    scale = HD ** (-0.5)
    q = q_ref[...]
    stacked = jnp.concatenate([q[:, j * HD:(j + 1) * HD] for j in range(GROUP)], axis=0)
    row = lax.broadcasted_iota(jnp.int32, (GROUP * BLK, BLK), 0) % BLK
    col = lax.broadcasted_iota(jnp.int32, (GROUP * BLK, BLK), 1)
    future = col > row
    run_max = jnp.full((GROUP * BLK, BLK), -jnp.inf, jnp.float32)
    for s in range(LIST):
        key = k_ref[0, slot_ref[local, s]]
        sc = lax.dot_general(
            stacked, key, (((1,), (1,)), ((), ())), preferred_element_type=jnp.float32
        ) * scale
        masked = jnp.logical_and(future, diag_ref[local, s] != 0)
        sc = jnp.where(masked, -jnp.inf, sc)
        score_sc[s] = sc
        run_max = jnp.maximum(run_max, sc)
    row_max = jnp.max(run_max, axis=1, keepdims=True)
    total = jnp.zeros((GROUP * BLK, BLK), jnp.float32)
    acc = jnp.zeros((GROUP * BLK, HD), jnp.float32)
    for s in range(LIST):
        powers = jnp.exp(score_sc[s] - row_max)
        total = total + powers
        value = v_ref[0, slot_ref[local, s]]
        acc = acc + jnp.dot(
            powers.astype(jnp.bfloat16), value, preferred_element_type=jnp.float32
        )
    denominator = jnp.sum(total, axis=1, keepdims=True)
    result = (acc / denominator).astype(jnp.bfloat16)
    o_ref[...] = jnp.concatenate(
        [result[j * BLK:(j + 1) * BLK] for j in range(GROUP)], axis=1
    )


def attend(slots, diag, queries, kv_buffer):
    blocks_here = queries.shape[0] // BLK
    buffer_blocks = kv_buffer.shape[1]
    flops = 4 * blocks_here * H * BLK * LIST * BLK * HD
    grid_spec = pltpu.PrefetchScalarGridSpec(
        num_scalar_prefetch=2,
        grid=(KVH, blocks_here),
        in_specs=[
            pl.BlockSpec((BLK, GROUP * HD), lambda g, b, *_: (b, g)),
            pl.BlockSpec((1, buffer_blocks, BLK, HD), lambda g, b, *_: (0, 0, 0, g)),
            pl.BlockSpec((1, buffer_blocks, BLK, HD), lambda g, b, *_: (1, 0, 0, g)),
        ],
        out_specs=pl.BlockSpec((BLK, GROUP * HD), lambda g, b, *_: (b, g)),
        scratch_shapes=[pltpu.VMEM((LIST, GROUP * BLK, BLK), jnp.float32)],
    )
    return pl.pallas_call(
        attend_kernel,
        out_shape=jax.ShapeDtypeStruct(queries.shape, jnp.bfloat16),
        grid_spec=grid_spec,
        compiler_params=pltpu.CompilerParams(
            dimension_semantics=("arbitrary", "arbitrary"),
        ),
        cost_estimate=pl.CostEstimate(
            flops=flops,
            transcendentals=blocks_here * H * BLK * LIST * BLK,
            bytes_accessed=2 * queries.size * 2 + kv_buffer.size * 2,
        ),
    )(slots, diag, queries, kv_buffer, kv_buffer)


def per_device(queries, key_rows, value_rows, pattern):
    tok_rows = queries.shape[0]
    blocks_here = tok_rows // BLK
    ctx_count = lax.axis_size("ctx")
    own_index = lax.axis_index("ctx")
    kv = jnp.stack([key_rows, value_rows])
    reach_rows = (WIN - 1) * BLK
    hops_back = (reach_rows + tok_rows - 1) // tok_rows
    early = []
    for offset in range(hops_back, 0, -1):
        need_rows = min(tok_rows, reach_rows - (offset - 1) * tok_rows)
        early.append(passed_along(kv[:, tok_rows - need_rows:], "ctx", offset))
    columns = blocks_here * ctx_count // STRIDE
    spread = STRIDE // blocks_here
    column_blocks = [
        tree_broadcast(kv[:, :BLK], "ctx", column * spread, ctx_count)
        for column in range(columns)
    ]
    buffer_blocks = columns + WIN - 1 + blocks_here
    kv_buffer = jnp.concatenate(column_blocks + early + [kv], axis=1).reshape(
        2, buffer_blocks, BLK, kv.shape[2]
    )
    first_block = own_index * blocks_here - (WIN - 1)
    rows_pattern = lax.dynamic_slice_in_dim(pattern, own_index * blocks_here, blocks_here, 0)
    in_window = jnp.arange(LIST, dtype=jnp.int32) < WIN
    slots = jnp.where(
        in_window[None, :],
        columns + rows_pattern - first_block,
        rows_pattern // STRIDE,
    )
    slots = jnp.clip(slots, 0, buffer_blocks - 1).astype(jnp.int32)
    blocks = own_index * blocks_here + jnp.arange(blocks_here, dtype=jnp.int32)
    diag = (rows_pattern == blocks[:, None]).astype(jnp.int32)
    return attend(slots, diag, queries, kv_buffer)


def solution(mesh):
    placed = (
        P(("groups", "ctx"), None),
        P(("groups", "ctx"), None),
        P(("groups", "ctx"), None),
        P(),
    )
    return jax.shard_map(
        per_device,
        mesh=mesh,
        in_specs=placed,
        out_specs=P(("groups", "ctx"), None),
        check_vma=False,
    )
```

```python
import functools

import jax
import jax.numpy as jnp
from jax import lax
from jax.experimental import pallas as pl
from jax.experimental.pallas import tpu as pltpu
from jax.sharding import PartitionSpec as P

H = 32
KVH = 8
HD = 128
BLK = 128
WIN = 8
STRIDE = 32
LIST = 11
GROUP = H // KVH


def shifted(shard, axis, by, sends):
    size = lax.axis_size(axis)
    pairs = [(i, i + by) for i in range(size) if sends(i) and 0 <= i + by < size]
    return lax.ppermute(shard, axis, pairs)


def window_blocks(kv, axis):
    index = lax.axis_index(axis)
    y_low = (index // 2) % 2 == 0
    core0 = index % 2 == 0
    back4 = shifted(kv, axis, 4, lambda i: True)
    up_y = shifted(kv, axis, 2, lambda i: (i // 2) % 2 == 0)
    next_core = shifted(kv, axis, 1, lambda i: i % 2 == 0)
    down_y = shifted(back4, axis, -2, lambda i: (i // 2) % 2 == 1)
    back2 = jnp.where(y_low, down_y, up_y)
    partner_back4 = shifted(back4, axis, -1, lambda i: i % 2 == 1)
    size = lax.axis_size(axis)
    swap_pairs = [(i, i ^ 1) for i in range(size)]
    partner_back2 = lax.ppermute(back2, axis, swap_pairs)
    back3 = jnp.where(core0, partner_back4, partner_back2)
    back1 = jnp.where(core0, partner_back2, next_core)
    return [back4, back3, back2, back1]


def tree_broadcast(block, axis, source, size):
    index = lax.axis_index(axis)
    span = size - source
    held = block
    dist = 1
    while dist < span:
        dist *= 2
    dist //= 2
    while dist >= 1:
        pairs = [
            (source + j, source + j + dist)
            for j in range(0, span, 2 * dist)
            if j + dist < span
        ]
        got = lax.ppermute(held, axis, pairs)
        rel = index - source
        takes = (rel >= 0) & (rel % (2 * dist) == dist)
        held = jnp.where(takes, got, held)
        dist //= 2
    return held


def attend_kernel(slot_ref, diag_ref, q_ref, k_ref, v_ref, o_ref, score_sc):
    local = pl.program_id(1)
    scale = HD ** (-0.5)
    q = q_ref[...]
    stacked = jnp.concatenate([q[:, j * HD:(j + 1) * HD] for j in range(GROUP)], axis=0)
    row = lax.broadcasted_iota(jnp.int32, (GROUP * BLK, BLK), 0) % BLK
    col = lax.broadcasted_iota(jnp.int32, (GROUP * BLK, BLK), 1)
    future = col > row
    run_max = jnp.full((GROUP * BLK, BLK), -jnp.inf, jnp.float32)
    for s in range(LIST):
        key = k_ref[0, slot_ref[local, s]]
        sc = lax.dot_general(
            stacked, key, (((1,), (1,)), ((), ())), preferred_element_type=jnp.float32
        ) * scale
        masked = jnp.logical_and(future, diag_ref[local, s] != 0)
        sc = jnp.where(masked, -jnp.inf, sc)
        score_sc[s] = sc
        run_max = jnp.maximum(run_max, sc)
    row_max = jnp.max(run_max, axis=1, keepdims=True)
    total = jnp.zeros((GROUP * BLK, BLK), jnp.float32)
    acc = jnp.zeros((GROUP * BLK, HD), jnp.float32)
    for s in range(LIST):
        powers = jnp.exp(score_sc[s] - row_max)
        total = total + powers
        value = v_ref[0, slot_ref[local, s]]
        acc = acc + jnp.dot(
            powers.astype(jnp.bfloat16), value, preferred_element_type=jnp.float32
        )
    denominator = jnp.sum(total, axis=1, keepdims=True)
    result = (acc / denominator).astype(jnp.bfloat16)
    o_ref[...] = jnp.concatenate(
        [result[j * BLK:(j + 1) * BLK] for j in range(GROUP)], axis=1
    )


def attend(slots, diag, queries, kv_buffer):
    blocks_here = queries.shape[0] // BLK
    buffer_blocks = kv_buffer.shape[1]
    flops = 4 * blocks_here * H * BLK * LIST * BLK * HD
    grid_spec = pltpu.PrefetchScalarGridSpec(
        num_scalar_prefetch=2,
        grid=(KVH, blocks_here),
        in_specs=[
            pl.BlockSpec((BLK, GROUP * HD), lambda g, b, *_: (b, g)),
            pl.BlockSpec((1, buffer_blocks, BLK, HD), lambda g, b, *_: (0, 0, 0, g)),
            pl.BlockSpec((1, buffer_blocks, BLK, HD), lambda g, b, *_: (1, 0, 0, g)),
        ],
        out_specs=pl.BlockSpec((BLK, GROUP * HD), lambda g, b, *_: (b, g)),
        scratch_shapes=[pltpu.VMEM((LIST, GROUP * BLK, BLK), jnp.float32)],
    )
    return pl.pallas_call(
        attend_kernel,
        out_shape=jax.ShapeDtypeStruct(queries.shape, jnp.bfloat16),
        grid_spec=grid_spec,
        compiler_params=pltpu.CompilerParams(
            dimension_semantics=("arbitrary", "arbitrary"),
        ),
        cost_estimate=pl.CostEstimate(
            flops=flops,
            transcendentals=blocks_here * H * BLK * LIST * BLK,
            bytes_accessed=2 * queries.size * 2 + kv_buffer.size * 2,
        ),
    )(slots, diag, queries, kv_buffer, kv_buffer)


def per_device(queries, key_rows, value_rows, pattern):
    tok_rows = queries.shape[0]
    blocks_here = tok_rows // BLK
    ctx_count = lax.axis_size("ctx")
    own_index = lax.axis_index("ctx")
    kv = jnp.stack([key_rows, value_rows])
    assert blocks_here == 2 and ctx_count % 4 == 0
    early = window_blocks(kv, "ctx")
    columns = blocks_here * ctx_count // STRIDE
    spread = STRIDE // blocks_here
    column_blocks = [
        tree_broadcast(kv[:, :BLK], "ctx", column * spread, ctx_count)
        for column in range(columns)
    ]
    buffer_blocks = columns + 4 * blocks_here + blocks_here
    kv_buffer = jnp.concatenate(column_blocks + early + [kv], axis=1).reshape(
        2, buffer_blocks, BLK, kv.shape[2]
    )
    first_block = own_index * blocks_here - 4 * blocks_here
    rows_pattern = lax.dynamic_slice_in_dim(pattern, own_index * blocks_here, blocks_here, 0)
    slots = jnp.where(
        rows_pattern >= first_block,
        columns + rows_pattern - first_block,
        rows_pattern // STRIDE,
    )
    slots = jnp.clip(slots, 0, buffer_blocks - 1).astype(jnp.int32)
    blocks = own_index * blocks_here + jnp.arange(blocks_here, dtype=jnp.int32)
    diag = (rows_pattern == blocks[:, None]).astype(jnp.int32)
    return attend(slots, diag, queries, kv_buffer)


def solution(mesh):
    placed = (
        P(("groups", "ctx"), None),
        P(("groups", "ctx"), None),
        P(("groups", "ctx"), None),
        P(),
    )
    return jax.shard_map(
        per_device,
        mesh=mesh,
        in_specs=placed,
        out_specs=P(("groups", "ctx"), None),
        check_vma=False,
    )
```

```python
import functools

import jax
import jax.numpy as jnp
from jax import lax
from jax.experimental import pallas as pl
from jax.experimental.pallas import tpu as pltpu
from jax.sharding import PartitionSpec as P

H = 32
KVH = 8
HD = 128
BLK = 128
WIN = 8
STRIDE = 32
LIST = 11
GROUP = H // KVH


def shifted(shard, axis, by, sends):
    size = lax.axis_size(axis)
    pairs = [(i, i + by) for i in range(size) if sends(i) and 0 <= i + by < size]
    return lax.ppermute(shard, axis, pairs)


def window_blocks(kv, axis):
    index = lax.axis_index(axis)
    size = lax.axis_size(axis)
    y_low = (index // 2) % 2 == 0
    core0 = index % 2 == 0
    swap_pairs = [(i, i ^ 1) for i in range(size)]
    up_y = shifted(kv, axis, 2, lambda i: (i // 2) % 2 == 0)
    later = kv[:, BLK:]
    pieces = {"back4": [], "back3": [], "back2": [], "back1": []}
    for half in range(2):
        own = kv[:, half * BLK:(half + 1) * BLK]
        if half == 1:
            own, pieces["back4"][0] = lax.optimization_barrier((later, pieces["back4"][0]))
        back4 = shifted(own, axis, 4, lambda i: True)
        down_y = shifted(back4, axis, -2, lambda i: (i // 2) % 2 == 1)
        back2 = jnp.where(y_low, down_y, up_y[:, half * BLK:(half + 1) * BLK])
        sent = jnp.stack([jnp.where(core0, own, back4), back2])
        got = lax.ppermute(sent, axis, swap_pairs)
        pieces["back4"].append(back4)
        pieces["back3"].append(jnp.where(core0, got[0], got[1]))
        pieces["back2"].append(back2)
        pieces["back1"].append(jnp.where(core0, got[1], got[0]))
    return pieces["back4"] + pieces["back3"] + pieces["back2"] + pieces["back1"]


def tree_broadcast(block, axis, source, size):
    index = lax.axis_index(axis)
    span = size - source
    held = block
    dist = 1
    while dist < span:
        dist *= 2
    dist //= 2
    while dist >= 1:
        pairs = [
            (source + j, source + j + dist)
            for j in range(0, span, 2 * dist)
            if j + dist < span
        ]
        got = lax.ppermute(held, axis, pairs)
        rel = index - source
        takes = (rel >= 0) & (rel % (2 * dist) == dist)
        held = jnp.where(takes, got, held)
        dist //= 2
    return held


def attend_kernel(slot_ref, diag_ref, q_ref, k_ref, v_ref, o_ref, score_sc):
    local = pl.program_id(1)
    scale = HD ** (-0.5)
    q = q_ref[...]
    stacked = jnp.concatenate([q[:, j * HD:(j + 1) * HD] for j in range(GROUP)], axis=0)
    row = lax.broadcasted_iota(jnp.int32, (GROUP * BLK, BLK), 0) % BLK
    col = lax.broadcasted_iota(jnp.int32, (GROUP * BLK, BLK), 1)
    future = col > row
    run_max = jnp.full((GROUP * BLK, BLK), -jnp.inf, jnp.float32)
    for s in range(LIST):
        key = k_ref[0, slot_ref[local, s]]
        sc = lax.dot_general(
            stacked, key, (((1,), (1,)), ((), ())), preferred_element_type=jnp.float32
        ) * scale
        sc = lax.cond(
            diag_ref[local, s] != 0,
            lambda x: jnp.where(future, -jnp.inf, x),
            lambda x: x,
            sc,
        )
        score_sc[s] = sc
        run_max = jnp.maximum(run_max, sc)
    row_max = jnp.max(run_max, axis=1, keepdims=True)
    total = jnp.zeros((GROUP * BLK, BLK), jnp.float32)
    acc = jnp.zeros((GROUP * BLK, HD), jnp.float32)
    for s in range(LIST):
        powers = jnp.exp(score_sc[s] - row_max)
        total = total + powers
        value = v_ref[0, slot_ref[local, s]]
        acc = acc + jnp.dot(
            powers.astype(jnp.bfloat16), value, preferred_element_type=jnp.float32
        )
    denominator = jnp.sum(total, axis=1, keepdims=True)
    result = (acc / denominator).astype(jnp.bfloat16)
    o_ref[...] = jnp.concatenate(
        [result[j * BLK:(j + 1) * BLK] for j in range(GROUP)], axis=1
    )


def attend(slots, diag, queries, kv_buffer):
    blocks_here = queries.shape[0] // BLK
    buffer_blocks = kv_buffer.shape[1]
    flops = 4 * blocks_here * H * BLK * LIST * BLK * HD
    grid_spec = pltpu.PrefetchScalarGridSpec(
        num_scalar_prefetch=2,
        grid=(KVH, blocks_here),
        in_specs=[
            pl.BlockSpec((BLK, GROUP * HD), lambda g, b, *_: (b, g)),
            pl.BlockSpec((1, buffer_blocks, BLK, HD), lambda g, b, *_: (0, 0, 0, g)),
            pl.BlockSpec((1, buffer_blocks, BLK, HD), lambda g, b, *_: (1, 0, 0, g)),
        ],
        out_specs=pl.BlockSpec((BLK, GROUP * HD), lambda g, b, *_: (b, g)),
        scratch_shapes=[pltpu.VMEM((LIST, GROUP * BLK, BLK), jnp.float32)],
    )
    return pl.pallas_call(
        attend_kernel,
        out_shape=jax.ShapeDtypeStruct(queries.shape, jnp.bfloat16),
        grid_spec=grid_spec,
        compiler_params=pltpu.CompilerParams(
            dimension_semantics=("arbitrary", "arbitrary"),
        ),
        cost_estimate=pl.CostEstimate(
            flops=flops,
            transcendentals=blocks_here * H * BLK * LIST * BLK,
            bytes_accessed=2 * queries.size * 2 + kv_buffer.size * 2,
        ),
    )(slots, diag, queries, kv_buffer, kv_buffer)


def per_device(queries, key_rows, value_rows, pattern):
    tok_rows = queries.shape[0]
    blocks_here = tok_rows // BLK
    ctx_count = lax.axis_size("ctx")
    own_index = lax.axis_index("ctx")
    kv = jnp.stack([key_rows, value_rows])
    assert blocks_here == 2 and ctx_count % 4 == 0
    early = window_blocks(kv, "ctx")
    columns = blocks_here * ctx_count // STRIDE
    spread = STRIDE // blocks_here
    column_blocks = [
        tree_broadcast(kv[:, :BLK], "ctx", column * spread, ctx_count)
        for column in range(columns)
    ]
    buffer_blocks = columns + 4 * blocks_here + blocks_here
    kv_buffer = jnp.concatenate(column_blocks + early + [kv], axis=1).reshape(
        2, buffer_blocks, BLK, kv.shape[2]
    )
    first_block = own_index * blocks_here - 4 * blocks_here
    rows_pattern = lax.dynamic_slice_in_dim(pattern, own_index * blocks_here, blocks_here, 0)
    slots = jnp.where(
        rows_pattern >= first_block,
        columns + rows_pattern - first_block,
        rows_pattern // STRIDE,
    )
    slots = jnp.clip(slots, 0, buffer_blocks - 1).astype(jnp.int32)
    blocks = own_index * blocks_here + jnp.arange(blocks_here, dtype=jnp.int32)
    diag = (rows_pattern == blocks[:, None]).astype(jnp.int32)
    return attend(slots, diag, queries, kv_buffer)


def solution(mesh):
    placed = (
        P(("groups", "ctx"), None),
        P(("groups", "ctx"), None),
        P(("groups", "ctx"), None),
        P(),
    )
    return jax.shard_map(
        per_device,
        mesh=mesh,
        in_specs=placed,
        out_specs=P(("groups", "ctx"), None),
        check_vma=False,
    )
```

```python
import functools

import jax
import jax.numpy as jnp
from jax import lax
from jax.experimental import pallas as pl
from jax.experimental.pallas import tpu as pltpu
from jax.sharding import PartitionSpec as P

H = 32
KVH = 8
HD = 128
BLK = 128
WIN = 8
STRIDE = 32
LIST = 11
GROUP = H // KVH


def shifted(shard, axis, by, sends):
    size = lax.axis_size(axis)
    pairs = [(i, i + by) for i in range(size) if sends(i) and 0 <= i + by < size]
    return lax.ppermute(shard, axis, pairs)


def window_blocks(kv, axis):
    index = lax.axis_index(axis)
    y_low = (index // 2) % 2 == 0
    core0 = index % 2 == 0
    back4 = shifted(kv, axis, 4, lambda i: True)
    up_y = shifted(kv, axis, 2, lambda i: (i // 2) % 2 == 0)
    next_core = shifted(kv, axis, 1, lambda i: i % 2 == 0)
    down_y = shifted(back4, axis, -2, lambda i: (i // 2) % 2 == 1)
    back2 = jnp.where(y_low, down_y, up_y)
    partner_back4 = shifted(back4, axis, -1, lambda i: i % 2 == 1)
    size = lax.axis_size(axis)
    swap_pairs = [(i, i ^ 1) for i in range(size)]
    partner_back2 = lax.ppermute(back2, axis, swap_pairs)
    back3 = jnp.where(core0, partner_back4, partner_back2)
    back1 = jnp.where(core0, partner_back2, next_core)
    return [back4, back3, back2, back1]


def tree_broadcast(block, axis, source, size):
    index = lax.axis_index(axis)
    span = size - source
    held = block
    dist = 1
    while dist < span:
        dist *= 2
    dist //= 2
    while dist >= 1:
        pairs = [
            (source + j, source + j + dist)
            for j in range(0, span, 2 * dist)
            if j + dist < span
        ]
        got = lax.ppermute(held, axis, pairs)
        rel = index - source
        takes = (rel >= 0) & (rel % (2 * dist) == dist)
        held = jnp.where(takes, got, held)
        dist //= 2
    return held


def attend_kernel(slot_ref, diag_ref, q_ref, k_ref, v_ref, o_ref, score_sc, bias_sc):
    local = pl.program_id(1)
    exp2_scale = (HD ** (-0.5)) * 1.4426950408889634
    q = q_ref[...]
    stacked = jnp.concatenate([q[:, j * HD:(j + 1) * HD] for j in range(GROUP)], axis=0)
    row = lax.broadcasted_iota(jnp.int32, (GROUP * BLK, BLK), 0) % BLK
    col = lax.broadcasted_iota(jnp.int32, (GROUP * BLK, BLK), 1)
    bias_sc[0] = jnp.zeros((GROUP * BLK, BLK), jnp.float32)
    bias_sc[1] = jnp.where(col > row, -jnp.inf, 0.0).astype(jnp.float32)
    run_max = jnp.full((GROUP * BLK, BLK), -jnp.inf, jnp.float32)
    for s in range(LIST):
        key = k_ref[0, slot_ref[local, s]]
        sc = lax.dot_general(
            stacked, key, (((1,), (1,)), ((), ())), preferred_element_type=jnp.float32
        ) + bias_sc[diag_ref[local, s]]
        score_sc[s] = sc
        run_max = jnp.maximum(run_max, sc)
    row_max = jnp.max(run_max, axis=1, keepdims=True)
    total = jnp.zeros((GROUP * BLK, BLK), jnp.float32)
    acc = jnp.zeros((GROUP * BLK, HD), jnp.float32)
    for s in range(LIST):
        powers = jnp.exp2((score_sc[s] - row_max) * exp2_scale)
        total = total + powers
        value = v_ref[0, slot_ref[local, s]]
        acc = acc + jnp.dot(
            powers.astype(jnp.bfloat16), value, preferred_element_type=jnp.float32
        )
    denominator = jnp.sum(total, axis=1, keepdims=True)
    result = (acc / denominator).astype(jnp.bfloat16)
    o_ref[...] = jnp.concatenate(
        [result[j * BLK:(j + 1) * BLK] for j in range(GROUP)], axis=1
    )


def attend(slots, diag, queries, kv_buffer):
    blocks_here = queries.shape[0] // BLK
    buffer_blocks = kv_buffer.shape[1]
    flops = 4 * blocks_here * H * BLK * LIST * BLK * HD
    grid_spec = pltpu.PrefetchScalarGridSpec(
        num_scalar_prefetch=2,
        grid=(KVH, blocks_here),
        in_specs=[
            pl.BlockSpec((BLK, GROUP * HD), lambda g, b, *_: (b, g)),
            pl.BlockSpec((1, buffer_blocks, BLK, HD), lambda g, b, *_: (0, 0, 0, g)),
            pl.BlockSpec((1, buffer_blocks, BLK, HD), lambda g, b, *_: (1, 0, 0, g)),
        ],
        out_specs=pl.BlockSpec((BLK, GROUP * HD), lambda g, b, *_: (b, g)),
        scratch_shapes=[
            pltpu.VMEM((LIST, GROUP * BLK, BLK), jnp.float32),
            pltpu.VMEM((2, GROUP * BLK, BLK), jnp.float32),
        ],
    )
    return pl.pallas_call(
        attend_kernel,
        out_shape=jax.ShapeDtypeStruct(queries.shape, jnp.bfloat16),
        grid_spec=grid_spec,
        compiler_params=pltpu.CompilerParams(
            dimension_semantics=("arbitrary", "arbitrary"),
        ),
        cost_estimate=pl.CostEstimate(
            flops=flops,
            transcendentals=blocks_here * H * BLK * LIST * BLK,
            bytes_accessed=2 * queries.size * 2 + kv_buffer.size * 2,
        ),
    )(slots, diag, queries, kv_buffer, kv_buffer)


def per_device(queries, key_rows, value_rows, pattern):
    tok_rows = queries.shape[0]
    blocks_here = tok_rows // BLK
    ctx_count = lax.axis_size("ctx")
    own_index = lax.axis_index("ctx")
    kv = jnp.stack([key_rows, value_rows])
    assert blocks_here == 2 and ctx_count % 4 == 0
    early = window_blocks(kv, "ctx")
    columns = blocks_here * ctx_count // STRIDE
    spread = STRIDE // blocks_here
    column_blocks = [
        tree_broadcast(kv[:, :BLK], "ctx", column * spread, ctx_count)
        for column in range(columns)
    ]
    buffer_blocks = columns + 4 * blocks_here + blocks_here
    kv_buffer = jnp.concatenate(column_blocks + early + [kv], axis=1).reshape(
        2, buffer_blocks, BLK, kv.shape[2]
    )
    first_block = own_index * blocks_here - 4 * blocks_here
    rows_pattern = lax.dynamic_slice_in_dim(pattern, own_index * blocks_here, blocks_here, 0)
    slots = jnp.where(
        rows_pattern >= first_block,
        columns + rows_pattern - first_block,
        rows_pattern // STRIDE,
    )
    slots = jnp.clip(slots, 0, buffer_blocks - 1).astype(jnp.int32)
    blocks = own_index * blocks_here + jnp.arange(blocks_here, dtype=jnp.int32)
    diag = (rows_pattern == blocks[:, None]).astype(jnp.int32)
    return attend(slots, diag, queries, kv_buffer)


def solution(mesh):
    placed = (
        P(("groups", "ctx"), None),
        P(("groups", "ctx"), None),
        P(("groups", "ctx"), None),
        P(),
    )
    return jax.shard_map(
        per_device,
        mesh=mesh,
        in_specs=placed,
        out_specs=P(("groups", "ctx"), None),
        check_vma=False,
    )
```

```python
import functools

import jax
import jax.numpy as jnp
from jax import lax
from jax.experimental import pallas as pl
from jax.experimental.pallas import tpu as pltpu
from jax.sharding import PartitionSpec as P

H = 32
KVH = 8
HD = 128
BLK = 128
WIN = 8
STRIDE = 32
LIST = 11
GROUP = H // KVH


def shifted(shard, axis, by, sends):
    size = lax.axis_size(axis)
    pairs = [(i, i + by) for i in range(size) if sends(i) and 0 <= i + by < size]
    return lax.ppermute(shard, axis, pairs)


def window_blocks(kv, axis):
    index = lax.axis_index(axis)
    size = lax.axis_size(axis)
    y_low = (index // 2) % 2 == 0
    core0 = index % 2 == 0
    is_y_low = lambda i: (i // 2) % 2 == 0
    is_core0 = lambda i: i % 2 == 0
    back4_c0 = shifted(kv[:, BLK:], axis, 4, is_core0)
    back4_c1 = shifted(kv, axis, 4, lambda i: not is_core0(i))
    up_y = shifted(kv, axis, 2, is_y_low)
    down_first = shifted(kv, axis, -2, lambda i: is_core0(i) and not is_y_low(i))
    down_then_z = shifted(down_first, axis, 4, lambda i: is_core0(i) and is_y_low(i))
    z_then_down = shifted(back4_c1, axis, -2, lambda i: not is_core0(i) and not is_y_low(i))
    from_c0 = jnp.where(y_low, down_then_z, up_y)
    from_c1 = jnp.where(y_low, z_then_down, up_y)
    sent = jnp.where(
        core0, jnp.stack([from_c0, kv]), jnp.stack([back4_c1, from_c1])
    )
    got = lax.ppermute(sent, axis, [(i, i ^ 1) for i in range(size)])
    back4 = jnp.concatenate(
        [back4_c1[:, :BLK], jnp.where(core0, back4_c0, back4_c1[:, BLK:])], axis=1
    )
    back2 = jnp.where(core0, from_c0, from_c1)
    return [back4, got[0], back2, got[1]]


def tree_broadcast(block, axis, source, size):
    index = lax.axis_index(axis)
    span = size - source
    held = block
    dist = 1
    while dist < span:
        dist *= 2
    dist //= 2
    while dist >= 1:
        pairs = [
            (source + j, source + j + dist)
            for j in range(0, span, 2 * dist)
            if j + dist < span
        ]
        got = lax.ppermute(held, axis, pairs)
        rel = index - source
        takes = (rel >= 0) & (rel % (2 * dist) == dist)
        held = jnp.where(takes, got, held)
        dist //= 2
    return held


def attend_kernel(slot_ref, diag_ref, q_ref, k_ref, v_ref, o_ref, score_sc, bias_sc):
    local = pl.program_id(1)
    exp2_scale = (HD ** (-0.5)) * 1.4426950408889634
    q = q_ref[...]
    stacked = jnp.concatenate([q[:, j * HD:(j + 1) * HD] for j in range(GROUP)], axis=0)
    row = lax.broadcasted_iota(jnp.int32, (GROUP * BLK, BLK), 0) % BLK
    col = lax.broadcasted_iota(jnp.int32, (GROUP * BLK, BLK), 1)
    bias_sc[0] = jnp.zeros((GROUP * BLK, BLK), jnp.float32)
    bias_sc[1] = jnp.where(col > row, -jnp.inf, 0.0).astype(jnp.float32)
    run_max = jnp.full((GROUP * BLK, BLK), -jnp.inf, jnp.float32)
    for s in range(LIST):
        key = k_ref[0, slot_ref[local, s]]
        sc = lax.dot_general(
            stacked, key, (((1,), (1,)), ((), ())), preferred_element_type=jnp.float32
        ) + bias_sc[diag_ref[local, s]]
        score_sc[s] = sc
        run_max = jnp.maximum(run_max, sc)
    row_max = jnp.max(run_max, axis=1, keepdims=True)
    total = jnp.zeros((GROUP * BLK, BLK), jnp.float32)
    acc = jnp.zeros((GROUP * BLK, HD), jnp.float32)
    for s in range(LIST):
        powers = jnp.exp2((score_sc[s] - row_max) * exp2_scale)
        total = total + powers
        value = v_ref[0, slot_ref[local, s]]
        acc = acc + jnp.dot(
            powers.astype(jnp.bfloat16), value, preferred_element_type=jnp.float32
        )
    denominator = jnp.sum(total, axis=1, keepdims=True)
    result = (acc / denominator).astype(jnp.bfloat16)
    o_ref[...] = jnp.concatenate(
        [result[j * BLK:(j + 1) * BLK] for j in range(GROUP)], axis=1
    )


def attend(slots, diag, queries, kv_buffer):
    blocks_here = queries.shape[0] // BLK
    buffer_blocks = kv_buffer.shape[1]
    flops = 4 * blocks_here * H * BLK * LIST * BLK * HD
    grid_spec = pltpu.PrefetchScalarGridSpec(
        num_scalar_prefetch=2,
        grid=(KVH, blocks_here),
        in_specs=[
            pl.BlockSpec((BLK, GROUP * HD), lambda g, b, *_: (b, g)),
            pl.BlockSpec((1, buffer_blocks, BLK, HD), lambda g, b, *_: (0, 0, 0, g)),
            pl.BlockSpec((1, buffer_blocks, BLK, HD), lambda g, b, *_: (1, 0, 0, g)),
        ],
        out_specs=pl.BlockSpec((BLK, GROUP * HD), lambda g, b, *_: (b, g)),
        scratch_shapes=[
            pltpu.VMEM((LIST, GROUP * BLK, BLK), jnp.float32),
            pltpu.VMEM((2, GROUP * BLK, BLK), jnp.float32),
        ],
    )
    return pl.pallas_call(
        attend_kernel,
        out_shape=jax.ShapeDtypeStruct(queries.shape, jnp.bfloat16),
        grid_spec=grid_spec,
        compiler_params=pltpu.CompilerParams(
            dimension_semantics=("arbitrary", "arbitrary"),
        ),
        cost_estimate=pl.CostEstimate(
            flops=flops,
            transcendentals=blocks_here * H * BLK * LIST * BLK,
            bytes_accessed=2 * queries.size * 2 + kv_buffer.size * 2,
        ),
    )(slots, diag, queries, kv_buffer, kv_buffer)


def per_device(queries, key_rows, value_rows, pattern):
    tok_rows = queries.shape[0]
    blocks_here = tok_rows // BLK
    ctx_count = lax.axis_size("ctx")
    own_index = lax.axis_index("ctx")
    kv = jnp.stack([key_rows, value_rows])
    assert blocks_here == 2 and ctx_count % 4 == 0
    early = window_blocks(kv, "ctx")
    columns = blocks_here * ctx_count // STRIDE
    spread = STRIDE // blocks_here
    column_blocks = [
        tree_broadcast(kv[:, :BLK], "ctx", column * spread, ctx_count)
        for column in range(columns)
    ]
    buffer_blocks = columns + 4 * blocks_here + blocks_here
    kv_buffer = jnp.concatenate(column_blocks + early + [kv], axis=1).reshape(
        2, buffer_blocks, BLK, kv.shape[2]
    )
    first_block = own_index * blocks_here - 4 * blocks_here
    rows_pattern = lax.dynamic_slice_in_dim(pattern, own_index * blocks_here, blocks_here, 0)
    slots = jnp.where(
        rows_pattern > first_block,
        columns + rows_pattern - first_block,
        rows_pattern // STRIDE,
    )
    slots = jnp.clip(slots, 0, buffer_blocks - 1).astype(jnp.int32)
    blocks = own_index * blocks_here + jnp.arange(blocks_here, dtype=jnp.int32)
    diag = (rows_pattern == blocks[:, None]).astype(jnp.int32)
    return attend(slots, diag, queries, kv_buffer)


def solution(mesh):
    placed = (
        P(("groups", "ctx"), None),
        P(("groups", "ctx"), None),
        P(("groups", "ctx"), None),
        P(),
    )
    return jax.shard_map(
        per_device,
        mesh=mesh,
        in_specs=placed,
        out_specs=P(("groups", "ctx"), None),
        check_vma=False,
    )
```

```python
import functools

import jax
import jax.numpy as jnp
from jax import lax
from jax.experimental import pallas as pl
from jax.experimental.pallas import tpu as pltpu
from jax.sharding import PartitionSpec as P

H = 32
KVH = 8
HD = 128
BLK = 128
WIN = 8
STRIDE = 32
LIST = 11
GROUP = H // KVH


def shifted(shard, axis, by, sends):
    size = lax.axis_size(axis)
    pairs = [(i, i + by) for i in range(size) if sends(i) and 0 <= i + by < size]
    return lax.ppermute(shard, axis, pairs)


def window_blocks(kv, axis):
    index = lax.axis_index(axis)
    y_low = (index // 2) % 2 == 0
    core0 = index % 2 == 0
    back4 = shifted(kv, axis, 4, lambda i: True)
    up_y = shifted(kv, axis, 2, lambda i: (i // 2) % 2 == 0)
    next_core = shifted(kv, axis, 1, lambda i: i % 2 == 0)
    down_y = shifted(back4, axis, -2, lambda i: (i // 2) % 2 == 1)
    back2 = jnp.where(y_low, down_y, up_y)
    partner_back4 = shifted(back4, axis, -1, lambda i: i % 2 == 1)
    size = lax.axis_size(axis)
    swap_pairs = [(i, i ^ 1) for i in range(size)]
    partner_back2 = lax.ppermute(back2, axis, swap_pairs)
    back3 = jnp.where(core0, partner_back4, partner_back2)
    back1 = jnp.where(core0, partner_back2, next_core)
    return [back4, back3, back2, back1]


def tree_broadcast(block, axis, source, size):
    index = lax.axis_index(axis)
    span = size - source
    held = block
    dist = 1
    while dist < span:
        dist *= 2
    dist //= 2
    while dist >= 1:
        pairs = [
            (source + j, source + j + dist)
            for j in range(0, span, 2 * dist)
            if j + dist < span
        ]
        got = lax.ppermute(held, axis, pairs)
        rel = index - source
        takes = (rel >= 0) & (rel % (2 * dist) == dist)
        held = jnp.where(takes, got, held)
        dist //= 2
    return held


def attend_kernel(slot_ref, diag_ref, q_ref, k_ref, v_ref, o_ref, score_sc, bias_sc):
    local = pl.program_id(1)
    exp2_scale = (HD ** (-0.5)) * 1.4426950408889634
    q = q_ref[...]
    stacked = jnp.concatenate([q[:, j * HD:(j + 1) * HD] for j in range(GROUP)], axis=0)
    row = lax.broadcasted_iota(jnp.int32, (GROUP * BLK, BLK), 0) % BLK
    col = lax.broadcasted_iota(jnp.int32, (GROUP * BLK, BLK), 1)
    bias_sc[0] = jnp.zeros((GROUP * BLK, BLK), jnp.float32)
    bias_sc[1] = jnp.where(col > row, -jnp.inf, 0.0).astype(jnp.float32)
    run_max = jnp.full((GROUP * BLK, BLK), -jnp.inf, jnp.float32)
    for s in range(LIST):
        key = k_ref[0, slot_ref[local, s]]
        sc = lax.dot_general(
            stacked, key, (((1,), (1,)), ((), ())), preferred_element_type=jnp.float32
        ) + bias_sc[diag_ref[local, s]]
        score_sc[s] = sc
        run_max = jnp.maximum(run_max, sc)
    row_max = jnp.max(run_max, axis=1, keepdims=True)
    total = jnp.zeros((GROUP * BLK, BLK), jnp.float32)
    acc = jnp.zeros((GROUP * BLK, HD), jnp.float32)
    for s in range(LIST):
        powers = jnp.exp2((score_sc[s] - row_max) * exp2_scale)
        total = total + powers
        value = v_ref[0, slot_ref[local, s]]
        acc = acc + jnp.dot(
            powers.astype(jnp.bfloat16), value, preferred_element_type=jnp.float32
        )
    denominator = jnp.sum(total, axis=1, keepdims=True)
    result = (acc / denominator).astype(jnp.bfloat16)
    o_ref[...] = jnp.concatenate(
        [result[j * BLK:(j + 1) * BLK] for j in range(GROUP)], axis=1
    )


def attend(slots, diag, queries, kv_buffer):
    blocks_here = queries.shape[0] // BLK
    buffer_blocks = kv_buffer.shape[1]
    flops = 4 * blocks_here * H * BLK * LIST * BLK * HD
    grid_spec = pltpu.PrefetchScalarGridSpec(
        num_scalar_prefetch=2,
        grid=(KVH, blocks_here),
        in_specs=[
            pl.BlockSpec((BLK, GROUP * HD), lambda g, b, *_: (b, g)),
            pl.BlockSpec((1, buffer_blocks, BLK, HD), lambda g, b, *_: (0, 0, 0, g)),
            pl.BlockSpec((1, buffer_blocks, BLK, HD), lambda g, b, *_: (1, 0, 0, g)),
        ],
        out_specs=pl.BlockSpec((BLK, GROUP * HD), lambda g, b, *_: (b, g)),
        scratch_shapes=[
            pltpu.VMEM((LIST, GROUP * BLK, BLK), jnp.float32),
            pltpu.VMEM((2, GROUP * BLK, BLK), jnp.float32),
        ],
    )
    return pl.pallas_call(
        attend_kernel,
        out_shape=jax.ShapeDtypeStruct(queries.shape, jnp.bfloat16),
        grid_spec=grid_spec,
        compiler_params=pltpu.CompilerParams(
            dimension_semantics=("arbitrary", "arbitrary"),
            vmem_limit_bytes=24 * 1024 * 1024,
        ),
        cost_estimate=pl.CostEstimate(
            flops=flops,
            transcendentals=blocks_here * H * BLK * LIST * BLK,
            bytes_accessed=2 * queries.size * 2 + kv_buffer.size * 2,
        ),
    )(slots, diag, queries, kv_buffer, kv_buffer)


def per_device(queries, key_rows, value_rows, pattern):
    tok_rows = queries.shape[0]
    blocks_here = tok_rows // BLK
    ctx_count = lax.axis_size("ctx")
    own_index = lax.axis_index("ctx")
    kv = jnp.stack([key_rows, value_rows])
    assert blocks_here == 2 and ctx_count % 4 == 0
    early = window_blocks(kv, "ctx")
    columns = blocks_here * ctx_count // STRIDE
    spread = STRIDE // blocks_here
    column_blocks = [
        tree_broadcast(kv[:, :BLK], "ctx", column * spread, ctx_count)
        for column in range(columns)
    ]
    buffer_blocks = columns + 4 * blocks_here + blocks_here
    kv_buffer = jnp.concatenate(column_blocks + early + [kv], axis=1).reshape(
        2, buffer_blocks, BLK, kv.shape[2]
    )
    first_block = own_index * blocks_here - 4 * blocks_here
    rows_pattern = lax.dynamic_slice_in_dim(pattern, own_index * blocks_here, blocks_here, 0)
    slots = jnp.where(
        rows_pattern >= first_block,
        columns + rows_pattern - first_block,
        rows_pattern // STRIDE,
    )
    slots = jnp.clip(slots, 0, buffer_blocks - 1).astype(jnp.int32)
    blocks = own_index * blocks_here + jnp.arange(blocks_here, dtype=jnp.int32)
    diag = (rows_pattern == blocks[:, None]).astype(jnp.int32)
    return attend(slots, diag, queries, kv_buffer)


def solution(mesh):
    placed = (
        P(("groups", "ctx"), None),
        P(("groups", "ctx"), None),
        P(("groups", "ctx"), None),
        P(),
    )
    return jax.shard_map(
        per_device,
        mesh=mesh,
        in_specs=placed,
        out_specs=P(("groups", "ctx"), None),
        check_vma=False,
    )
```

```python
import functools

import jax
import jax.numpy as jnp
from jax import lax
from jax.experimental import pallas as pl
from jax.experimental.pallas import tpu as pltpu
from jax.sharding import PartitionSpec as P

H = 32
KVH = 8
HD = 128
BLK = 128
WIN = 8
STRIDE = 32
LIST = 11
GROUP = H // KVH


def shifted(shard, axis, by, sends):
    size = lax.axis_size(axis)
    pairs = [(i, i + by) for i in range(size) if sends(i) and 0 <= i + by < size]
    return lax.ppermute(shard, axis, pairs)


def window_start(kv, axis, gate=None):
    if gate is not None:
        kv, gate = lax.optimization_barrier((kv, gate))
    back4 = shifted(kv, axis, 4, lambda i: True)
    up_y = shifted(kv, axis, 2, lambda i: (i // 2) % 2 == 0)
    next_core = shifted(kv, axis, 1, lambda i: i % 2 == 0)
    down_y = shifted(back4, axis, -2, lambda i: (i // 2) % 2 == 1)
    partner_back4 = shifted(back4, axis, -1, lambda i: i % 2 == 1)
    return back4, up_y, next_core, down_y, partner_back4


def window_finish(started, axis, hold=None):
    back4, up_y, next_core, down_y, partner_back4 = started
    index = lax.axis_index(axis)
    size = lax.axis_size(axis)
    y_low = (index // 2) % 2 == 0
    core0 = index % 2 == 0
    if hold is not None:
        down_y, hold = lax.optimization_barrier((down_y, hold))
    back2 = jnp.where(y_low, down_y, up_y)
    swap_pairs = [(i, i ^ 1) for i in range(size)]
    partner_back2 = lax.ppermute(back2, axis, swap_pairs)
    back3 = jnp.where(core0, partner_back4, partner_back2)
    back1 = jnp.where(core0, partner_back2, next_core)
    return [back4, back3, back2, back1], hold


def tree_broadcast(block, axis, source, size):
    index = lax.axis_index(axis)
    span = size - source
    held = block
    dist = 1
    while dist < span:
        dist *= 2
    dist //= 2
    while dist >= 1:
        pairs = [
            (source + j, source + j + dist)
            for j in range(0, span, 2 * dist)
            if j + dist < span
        ]
        got = lax.ppermute(held, axis, pairs)
        rel = index - source
        takes = (rel >= 0) & (rel % (2 * dist) == dist)
        held = jnp.where(takes, got, held)
        dist //= 2
    return held


def attend_kernel(slot_ref, diag_ref, q_ref, k_ref, v_ref, o_ref, score_sc, bias_sc):
    local = pl.program_id(1)
    exp2_scale = (HD ** (-0.5)) * 1.4426950408889634
    q = q_ref[...]
    stacked = jnp.concatenate([q[:, j * HD:(j + 1) * HD] for j in range(GROUP)], axis=0)
    row = lax.broadcasted_iota(jnp.int32, (GROUP * BLK, BLK), 0) % BLK
    col = lax.broadcasted_iota(jnp.int32, (GROUP * BLK, BLK), 1)
    bias_sc[0] = jnp.zeros((GROUP * BLK, BLK), jnp.float32)
    bias_sc[1] = jnp.where(col > row, -jnp.inf, 0.0).astype(jnp.float32)
    run_max = jnp.full((GROUP * BLK, BLK), -jnp.inf, jnp.float32)
    for s in range(LIST):
        key = k_ref[0, slot_ref[local, s]]
        sc = lax.dot_general(
            stacked, key, (((1,), (1,)), ((), ())), preferred_element_type=jnp.float32
        ) + bias_sc[diag_ref[local, s]]
        score_sc[s] = sc
        run_max = jnp.maximum(run_max, sc)
    row_max = jnp.max(run_max, axis=1, keepdims=True)
    total = jnp.zeros((GROUP * BLK, BLK), jnp.float32)
    acc = jnp.zeros((GROUP * BLK, HD), jnp.float32)
    for s in range(LIST):
        powers = jnp.exp2((score_sc[s] - row_max) * exp2_scale)
        total = total + powers
        value = v_ref[0, slot_ref[local, s]]
        acc = acc + jnp.dot(
            powers.astype(jnp.bfloat16), value, preferred_element_type=jnp.float32
        )
    denominator = jnp.sum(total, axis=1, keepdims=True)
    result = (acc / denominator).astype(jnp.bfloat16)
    o_ref[...] = jnp.concatenate(
        [result[j * BLK:(j + 1) * BLK] for j in range(GROUP)], axis=1
    )


def attend(slots, diag, queries, kv_buffer, first_head, into=None):
    blocks_here = queries.shape[0] // BLK
    buffer_blocks = kv_buffer.shape[1]
    heads = kv_buffer.shape[3] // HD
    flops = 4 * blocks_here * heads * GROUP * BLK * LIST * BLK * HD
    head_block = first_head
    in_specs = [
        pl.BlockSpec((BLK, GROUP * HD), lambda g, b, *_: (b, g + head_block)),
        pl.BlockSpec((1, buffer_blocks, BLK, HD), lambda g, b, *_: (0, 0, 0, g)),
        pl.BlockSpec((1, buffer_blocks, BLK, HD), lambda g, b, *_: (1, 0, 0, g)),
    ]
    operands = [slots, diag, queries, kv_buffer, kv_buffer]
    aliases = {}
    if into is not None:
        in_specs.append(pl.BlockSpec(memory_space=pl.ANY))
        operands.append(into)
        aliases = {len(operands) - 1: 0}
    grid_spec = pltpu.PrefetchScalarGridSpec(
        num_scalar_prefetch=2,
        grid=(heads, blocks_here),
        in_specs=in_specs,
        out_specs=pl.BlockSpec((BLK, GROUP * HD), lambda g, b, *_: (b, g + head_block)),
        scratch_shapes=[
            pltpu.VMEM((LIST, GROUP * BLK, BLK), jnp.float32),
            pltpu.VMEM((2, GROUP * BLK, BLK), jnp.float32),
        ],
    )
    kernel = attend_kernel if into is None else aliased_kernel
    return pl.pallas_call(
        kernel,
        out_shape=jax.ShapeDtypeStruct(queries.shape, jnp.bfloat16),
        grid_spec=grid_spec,
        input_output_aliases=aliases,
        compiler_params=pltpu.CompilerParams(
            dimension_semantics=("arbitrary", "arbitrary"),
            vmem_limit_bytes=24 * 1024 * 1024,
        ),
        cost_estimate=pl.CostEstimate(
            flops=flops,
            transcendentals=blocks_here * heads * GROUP * BLK * LIST * BLK,
            bytes_accessed=2 * queries.size * heads // KVH * 2 + kv_buffer.size * 2,
        ),
    )(*operands)


def aliased_kernel(slot_ref, diag_ref, q_ref, k_ref, v_ref, into_ref, o_ref, score_sc, bias_sc):
    attend_kernel(slot_ref, diag_ref, q_ref, k_ref, v_ref, o_ref, score_sc, bias_sc)


def per_device(queries, key_rows, value_rows, pattern):
    tok_rows = queries.shape[0]
    blocks_here = tok_rows // BLK
    ctx_count = lax.axis_size("ctx")
    own_index = lax.axis_index("ctx")
    kv = jnp.stack([key_rows, value_rows])
    assert blocks_here == 2 and ctx_count % 4 == 0
    columns = blocks_here * ctx_count // STRIDE
    spread = STRIDE // blocks_here
    column_blocks = [
        tree_broadcast(kv[:, :BLK], "ctx", column * spread, ctx_count)
        for column in range(columns)
    ]
    buffer_blocks = columns + 4 * blocks_here + blocks_here
    half = kv.shape[2] // 2
    chunks = [kv[:, :, :half], kv[:, :, half:]]
    first_started = window_start(chunks[0], "ctx")
    second_started = window_start(chunks[1], "ctx", gate=first_started[0])
    first, _ = window_finish(first_started, "ctx")

    def slab(pieces, part):
        cols = [c[:, :, part * half:(part + 1) * half] for c in column_blocks]
        return jnp.concatenate(cols + pieces + [chunks[part]], axis=1).reshape(
            2, buffer_blocks, BLK, half
        )

    first_block = own_index * blocks_here - 4 * blocks_here
    rows_pattern = lax.dynamic_slice_in_dim(pattern, own_index * blocks_here, blocks_here, 0)
    slots = jnp.where(
        rows_pattern >= first_block,
        columns + rows_pattern - first_block,
        rows_pattern // STRIDE,
    )
    slots = jnp.clip(slots, 0, buffer_blocks - 1).astype(jnp.int32)
    blocks = own_index * blocks_here + jnp.arange(blocks_here, dtype=jnp.int32)
    diag = (rows_pattern == blocks[:, None]).astype(jnp.int32)
    slab_first, _ = lax.optimization_barrier((slab(first, 0), second_started[0]))
    out = attend(slots, diag, queries, slab_first, 0)
    second, out = window_finish(second_started, "ctx", hold=out)
    return attend(slots, diag, queries, slab(second, 1), KVH // 2, into=out)


def solution(mesh):
    placed = (
        P(("groups", "ctx"), None),
        P(("groups", "ctx"), None),
        P(("groups", "ctx"), None),
        P(),
    )
    return jax.shard_map(
        per_device,
        mesh=mesh,
        in_specs=placed,
        out_specs=P(("groups", "ctx"), None),
        check_vma=False,
    )
```

```python
import functools

import jax
import jax.numpy as jnp
from jax import lax
from jax.experimental import pallas as pl
from jax.experimental.pallas import tpu as pltpu
from jax.sharding import PartitionSpec as P

H = 32
KVH = 8
HD = 128
BLK = 128
WIN = 8
STRIDE = 32
LIST = 11
GROUP = H // KVH


def shifted(shard, axis, by, sends):
    size = lax.axis_size(axis)
    pairs = [(i, i + by) for i in range(size) if sends(i) and 0 <= i + by < size]
    return lax.ppermute(shard, axis, pairs)


def window_blocks(kv, axis, extra=()):
    index = lax.axis_index(axis)
    y_low = (index // 2) % 2 == 0
    core0 = index % 2 == 0
    back4 = shifted(kv, axis, 4, lambda i: True)
    up_y = shifted(kv, axis, 2, lambda i: (i // 2) % 2 == 0)
    next_core = shifted(kv, axis, 1, lambda i: i % 2 == 0)
    down_y = shifted(back4, axis, -2, lambda i: (i // 2) % 2 == 1)
    back2 = jnp.where(y_low, down_y, up_y)
    partner_back4 = shifted(back4, axis, -1, lambda i: i % 2 == 1)
    size = lax.axis_size(axis)
    swap_pairs = [(i, i ^ 1) for i in range(size)]
    rows = back2.shape[1]
    sent = jnp.concatenate([back2] + list(extra), axis=1)
    got = lax.ppermute(sent, axis, swap_pairs)
    partner_back2 = got[:, :rows]
    partner_extra = [
        got[:, rows + k * BLK:rows + (k + 1) * BLK] for k in range(len(extra))
    ]
    back3 = jnp.where(core0, partner_back4, partner_back2)
    back1 = jnp.where(core0, partner_back2, next_core)
    return [back4, back3, back2, back1], partner_extra


def tree_broadcast(block, axis, source, size, last_round=True):
    index = lax.axis_index(axis)
    span = size - source
    held = block
    dist = 1
    while dist < span:
        dist *= 2
    dist //= 2
    while dist >= (1 if last_round else 2):
        pairs = [
            (source + j, source + j + dist)
            for j in range(0, span, 2 * dist)
            if j + dist < span
        ]
        got = lax.ppermute(held, axis, pairs)
        rel = index - source
        takes = (rel >= 0) & (rel % (2 * dist) == dist)
        held = jnp.where(takes, got, held)
        dist //= 2
    return held


def attend_kernel(slot_ref, diag_ref, q_ref, k_ref, v_ref, o_ref, score_sc, bias_sc):
    local = pl.program_id(1)
    exp2_scale = (HD ** (-0.5)) * 1.4426950408889634
    q = q_ref[...]
    stacked = jnp.concatenate([q[:, j * HD:(j + 1) * HD] for j in range(GROUP)], axis=0)
    row = lax.broadcasted_iota(jnp.int32, (GROUP * BLK, BLK), 0) % BLK
    col = lax.broadcasted_iota(jnp.int32, (GROUP * BLK, BLK), 1)
    bias_sc[0] = jnp.zeros((GROUP * BLK, BLK), jnp.float32)
    bias_sc[1] = jnp.where(col > row, -jnp.inf, 0.0).astype(jnp.float32)
    run_max = jnp.full((GROUP * BLK, BLK), -jnp.inf, jnp.float32)
    for s in range(LIST):
        key = k_ref[0, slot_ref[local, s]]
        sc = lax.dot_general(
            stacked, key, (((1,), (1,)), ((), ())), preferred_element_type=jnp.float32
        ) + bias_sc[diag_ref[local, s]]
        score_sc[s] = sc
        run_max = jnp.maximum(run_max, sc)
    row_max = jnp.max(run_max, axis=1, keepdims=True)
    total = jnp.zeros((GROUP * BLK, BLK), jnp.float32)
    acc = jnp.zeros((GROUP * BLK, HD), jnp.float32)
    for s in range(LIST):
        powers = jnp.exp2((score_sc[s] - row_max) * exp2_scale)
        total = total + powers
        value = v_ref[0, slot_ref[local, s]]
        acc = acc + jnp.dot(
            powers.astype(jnp.bfloat16), value, preferred_element_type=jnp.float32
        )
    denominator = jnp.sum(total, axis=1, keepdims=True)
    result = (acc / denominator).astype(jnp.bfloat16)
    o_ref[...] = jnp.concatenate(
        [result[j * BLK:(j + 1) * BLK] for j in range(GROUP)], axis=1
    )


def attend(slots, diag, queries, kv_buffer):
    blocks_here = queries.shape[0] // BLK
    buffer_blocks = kv_buffer.shape[1]
    flops = 4 * blocks_here * H * BLK * LIST * BLK * HD
    grid_spec = pltpu.PrefetchScalarGridSpec(
        num_scalar_prefetch=2,
        grid=(KVH, blocks_here),
        in_specs=[
            pl.BlockSpec((BLK, GROUP * HD), lambda g, b, *_: (b, g)),
            pl.BlockSpec((1, buffer_blocks, BLK, HD), lambda g, b, *_: (0, 0, 0, g)),
            pl.BlockSpec((1, buffer_blocks, BLK, HD), lambda g, b, *_: (1, 0, 0, g)),
        ],
        out_specs=pl.BlockSpec((BLK, GROUP * HD), lambda g, b, *_: (b, g)),
        scratch_shapes=[
            pltpu.VMEM((LIST, GROUP * BLK, BLK), jnp.float32),
            pltpu.VMEM((2, GROUP * BLK, BLK), jnp.float32),
        ],
    )
    return pl.pallas_call(
        attend_kernel,
        out_shape=jax.ShapeDtypeStruct(queries.shape, jnp.bfloat16),
        grid_spec=grid_spec,
        compiler_params=pltpu.CompilerParams(
            dimension_semantics=("arbitrary", "arbitrary"),
            vmem_limit_bytes=24 * 1024 * 1024,
        ),
        cost_estimate=pl.CostEstimate(
            flops=flops,
            transcendentals=blocks_here * H * BLK * LIST * BLK,
            bytes_accessed=2 * queries.size * 2 + kv_buffer.size * 2,
        ),
    )(slots, diag, queries, kv_buffer, kv_buffer)


def per_device(queries, key_rows, value_rows, pattern):
    tok_rows = queries.shape[0]
    blocks_here = tok_rows // BLK
    ctx_count = lax.axis_size("ctx")
    own_index = lax.axis_index("ctx")
    kv = jnp.stack([key_rows, value_rows])
    assert blocks_here == 2 and ctx_count % 4 == 0
    columns = blocks_here * ctx_count // STRIDE
    spread = STRIDE // blocks_here
    assert spread % 2 == 0
    held = [
        tree_broadcast(kv[:, :BLK], "ctx", column * spread, ctx_count, last_round=False)
        for column in range(columns)
    ]
    early, from_partner = window_blocks(kv, "ctx", extra=held)
    core0 = own_index % 2 == 0
    column_blocks = [jnp.where(core0, h, p) for h, p in zip(held, from_partner)]
    buffer_blocks = columns + 4 * blocks_here + blocks_here
    kv_buffer = jnp.concatenate(column_blocks + early + [kv], axis=1).reshape(
        2, buffer_blocks, BLK, kv.shape[2]
    )
    first_block = own_index * blocks_here - 4 * blocks_here
    rows_pattern = lax.dynamic_slice_in_dim(pattern, own_index * blocks_here, blocks_here, 0)
    slots = jnp.where(
        rows_pattern >= first_block,
        columns + rows_pattern - first_block,
        rows_pattern // STRIDE,
    )
    slots = jnp.clip(slots, 0, buffer_blocks - 1).astype(jnp.int32)
    blocks = own_index * blocks_here + jnp.arange(blocks_here, dtype=jnp.int32)
    diag = (rows_pattern == blocks[:, None]).astype(jnp.int32)
    return attend(slots, diag, queries, kv_buffer)


def solution(mesh):
    placed = (
        P(("groups", "ctx"), None),
        P(("groups", "ctx"), None),
        P(("groups", "ctx"), None),
        P(),
    )
    return jax.shard_map(
        per_device,
        mesh=mesh,
        in_specs=placed,
        out_specs=P(("groups", "ctx"), None),
        check_vma=False,
    )
```

```python
import functools

import jax
import jax.numpy as jnp
from jax import lax
from jax.experimental import pallas as pl
from jax.experimental.pallas import tpu as pltpu
from jax.sharding import PartitionSpec as P

H = 32
KVH = 8
HD = 128
BLK = 128
WIN = 8
STRIDE = 32
LIST = 11
GROUP = H // KVH


def shifted(shard, axis, by, sends):
    size = lax.axis_size(axis)
    pairs = [(i, i + by) for i in range(size) if sends(i) and 0 <= i + by < size]
    return lax.ppermute(shard, axis, pairs)


def window_start(kv, axis):
    back4 = shifted(kv, axis, 4, lambda i: True)
    up_y = shifted(kv, axis, 2, lambda i: (i // 2) % 2 == 0)
    next_core = shifted(kv, axis, 1, lambda i: i % 2 == 0)
    down_y = shifted(back4, axis, -2, lambda i: (i // 2) % 2 == 1)
    partner_back4 = shifted(back4, axis, -1, lambda i: i % 2 == 1)
    return back4, up_y, next_core, down_y, partner_back4


def window_finish(started, axis, extra=()):
    back4, up_y, next_core, down_y, partner_back4 = started
    index = lax.axis_index(axis)
    size = lax.axis_size(axis)
    y_low = (index // 2) % 2 == 0
    core0 = index % 2 == 0
    back2 = jnp.where(y_low, down_y, up_y)
    swap_pairs = [(i, i ^ 1) for i in range(size)]
    rows = back2.shape[1]
    sent = jnp.concatenate([back2] + list(extra), axis=1)
    got = lax.ppermute(sent, axis, swap_pairs)
    partner_back2 = got[:, :rows]
    partner_extra = [
        got[:, rows + k * BLK:rows + (k + 1) * BLK] for k in range(len(extra))
    ]
    back3 = jnp.where(core0, partner_back4, partner_back2)
    back1 = jnp.where(core0, partner_back2, next_core)
    return [back4, back3, back2, back1], partner_extra


def tree_broadcast(block, axis, source, size, last_round=True):
    index = lax.axis_index(axis)
    span = size - source
    held = block
    dist = 1
    while dist < span:
        dist *= 2
    dist //= 2
    while dist >= (1 if last_round else 2):
        pairs = [
            (source + j, source + j + dist)
            for j in range(0, span, 2 * dist)
            if j + dist < span
        ]
        got = lax.ppermute(held, axis, pairs)
        rel = index - source
        takes = (rel >= 0) & (rel % (2 * dist) == dist)
        held = jnp.where(takes, got, held)
        dist //= 2
    return held


def attend_kernel(slot_ref, diag_ref, q_ref, k_ref, v_ref, o_ref, score_sc, bias_sc):
    local = pl.program_id(1)
    exp2_scale = (HD ** (-0.5)) * 1.4426950408889634
    q = q_ref[...]
    stacked = jnp.concatenate([q[:, j * HD:(j + 1) * HD] for j in range(GROUP)], axis=0)
    row = lax.broadcasted_iota(jnp.int32, (GROUP * BLK, BLK), 0) % BLK
    col = lax.broadcasted_iota(jnp.int32, (GROUP * BLK, BLK), 1)
    bias_sc[0] = jnp.zeros((GROUP * BLK, BLK), jnp.float32)
    bias_sc[1] = jnp.where(col > row, -jnp.inf, 0.0).astype(jnp.float32)
    run_max = jnp.full((GROUP * BLK, BLK), -jnp.inf, jnp.float32)
    for s in range(LIST):
        key = k_ref[0, slot_ref[local, s]]
        sc = lax.dot_general(
            stacked, key, (((1,), (1,)), ((), ())), preferred_element_type=jnp.float32
        ) + bias_sc[diag_ref[local, s]]
        score_sc[s] = sc
        run_max = jnp.maximum(run_max, sc)
    row_max = jnp.max(run_max, axis=1, keepdims=True)
    total = jnp.zeros((GROUP * BLK, BLK), jnp.float32)
    acc = jnp.zeros((GROUP * BLK, HD), jnp.float32)
    for s in range(LIST):
        powers = jnp.exp2((score_sc[s] - row_max) * exp2_scale)
        total = total + powers
        value = v_ref[0, slot_ref[local, s]]
        acc = acc + jnp.dot(
            powers.astype(jnp.bfloat16), value, preferred_element_type=jnp.float32
        )
    denominator = jnp.sum(total, axis=1, keepdims=True)
    result = (acc / denominator).astype(jnp.bfloat16)
    o_ref[...] = jnp.concatenate(
        [result[j * BLK:(j + 1) * BLK] for j in range(GROUP)], axis=1
    )


def attend(slots, diag, queries, kv_buffer):
    blocks_here = queries.shape[0] // BLK
    buffer_blocks = kv_buffer.shape[1]
    flops = 4 * blocks_here * H * BLK * LIST * BLK * HD
    grid_spec = pltpu.PrefetchScalarGridSpec(
        num_scalar_prefetch=2,
        grid=(KVH, blocks_here),
        in_specs=[
            pl.BlockSpec((BLK, GROUP * HD), lambda g, b, *_: (b, g)),
            pl.BlockSpec((1, buffer_blocks, BLK, HD), lambda g, b, *_: (0, 0, 0, g)),
            pl.BlockSpec((1, buffer_blocks, BLK, HD), lambda g, b, *_: (1, 0, 0, g)),
        ],
        out_specs=pl.BlockSpec((BLK, GROUP * HD), lambda g, b, *_: (b, g)),
        scratch_shapes=[
            pltpu.VMEM((LIST, GROUP * BLK, BLK), jnp.float32),
            pltpu.VMEM((2, GROUP * BLK, BLK), jnp.float32),
        ],
    )
    return pl.pallas_call(
        attend_kernel,
        out_shape=jax.ShapeDtypeStruct(queries.shape, jnp.bfloat16),
        grid_spec=grid_spec,
        compiler_params=pltpu.CompilerParams(
            dimension_semantics=("arbitrary", "arbitrary"),
            vmem_limit_bytes=24 * 1024 * 1024,
        ),
        cost_estimate=pl.CostEstimate(
            flops=flops,
            transcendentals=blocks_here * H * BLK * LIST * BLK,
            bytes_accessed=2 * queries.size * 2 + kv_buffer.size * 2,
        ),
    )(slots, diag, queries, kv_buffer, kv_buffer)


def per_device(queries, key_rows, value_rows, pattern):
    tok_rows = queries.shape[0]
    blocks_here = tok_rows // BLK
    ctx_count = lax.axis_size("ctx")
    own_index = lax.axis_index("ctx")
    kv = jnp.stack([key_rows, value_rows])
    assert blocks_here == 2 and ctx_count % 4 == 0
    columns = blocks_here * ctx_count // STRIDE
    spread = STRIDE // blocks_here
    assert spread % 2 == 0
    started = window_start(kv, "ctx")
    first_rows, _, _ = lax.optimization_barrier((kv[:, :BLK], started[0], started[1]))
    held = [
        tree_broadcast(first_rows, "ctx", column * spread, ctx_count, last_round=False)
        for column in range(columns)
    ]
    early, from_partner = window_finish(started, "ctx", extra=held)
    core0 = own_index % 2 == 0
    column_blocks = [jnp.where(core0, h, p) for h, p in zip(held, from_partner)]
    buffer_blocks = columns + 4 * blocks_here + blocks_here
    kv_buffer = jnp.concatenate(column_blocks + early + [kv], axis=1).reshape(
        2, buffer_blocks, BLK, kv.shape[2]
    )
    first_block = own_index * blocks_here - 4 * blocks_here
    rows_pattern = lax.dynamic_slice_in_dim(pattern, own_index * blocks_here, blocks_here, 0)
    slots = jnp.where(
        rows_pattern >= first_block,
        columns + rows_pattern - first_block,
        rows_pattern // STRIDE,
    )
    slots = jnp.clip(slots, 0, buffer_blocks - 1).astype(jnp.int32)
    blocks = own_index * blocks_here + jnp.arange(blocks_here, dtype=jnp.int32)
    diag = (rows_pattern == blocks[:, None]).astype(jnp.int32)
    return attend(slots, diag, queries, kv_buffer)


def solution(mesh):
    placed = (
        P(("groups", "ctx"), None),
        P(("groups", "ctx"), None),
        P(("groups", "ctx"), None),
        P(),
    )
    return jax.shard_map(
        per_device,
        mesh=mesh,
        in_specs=placed,
        out_specs=P(("groups", "ctx"), None),
        check_vma=False,
    )
```

```python
import functools

import jax
import jax.numpy as jnp
from jax import lax
from jax.experimental import pallas as pl
from jax.experimental.pallas import tpu as pltpu
from jax.sharding import PartitionSpec as P

H = 32
KVH = 8
HD = 128
BLK = 128
WIN = 8
STRIDE = 32
LIST = 11
GROUP = H // KVH
PAIR = 2


def shifted(shard, axis, by, sends):
    size = lax.axis_size(axis)
    pairs = [(i, i + by) for i in range(size) if sends(i) and 0 <= i + by < size]
    return lax.ppermute(shard, axis, pairs)


def window_blocks(kv, axis):
    index = lax.axis_index(axis)
    y_low = (index // 2) % 2 == 0
    core0 = index % 2 == 0
    back4 = shifted(kv, axis, 4, lambda i: True)
    up_y = shifted(kv, axis, 2, lambda i: (i // 2) % 2 == 0)
    next_core = shifted(kv, axis, 1, lambda i: i % 2 == 0)
    down_y = shifted(back4, axis, -2, lambda i: (i // 2) % 2 == 1)
    back2 = jnp.where(y_low, down_y, up_y)
    partner_back4 = shifted(back4, axis, -1, lambda i: i % 2 == 1)
    size = lax.axis_size(axis)
    swap_pairs = [(i, i ^ 1) for i in range(size)]
    partner_back2 = lax.ppermute(back2, axis, swap_pairs)
    back3 = jnp.where(core0, partner_back4, partner_back2)
    back1 = jnp.where(core0, partner_back2, next_core)
    return [back4, back3, back2, back1]


def tree_broadcast(block, axis, source, size):
    index = lax.axis_index(axis)
    span = size - source
    held = block
    dist = 1
    while dist < span:
        dist *= 2
    dist //= 2
    while dist >= 1:
        pairs = [
            (source + j, source + j + dist)
            for j in range(0, span, 2 * dist)
            if j + dist < span
        ]
        got = lax.ppermute(held, axis, pairs)
        rel = index - source
        takes = (rel >= 0) & (rel % (2 * dist) == dist)
        held = jnp.where(takes, got, held)
        dist //= 2
    return held


def attend_kernel(slot_ref, diag_ref, q_ref, k_ref, v_ref, o_ref, score_sc, bias_sc):
    local = pl.program_id(1)
    exp2_scale = (HD ** (-0.5)) * 1.4426950408889634
    rows = PAIR * BLK
    row = lax.broadcasted_iota(jnp.int32, (rows, BLK), 0) % BLK
    col = lax.broadcasted_iota(jnp.int32, (rows, BLK), 1)
    bias_sc[0] = jnp.zeros((rows, BLK), jnp.float32)
    bias_sc[1] = jnp.where(col > row, -jnp.inf, 0.0).astype(jnp.float32)
    q = q_ref[...]
    for half in range(GROUP // PAIR):
        heads = range(half * PAIR, (half + 1) * PAIR)
        stacked = jnp.concatenate([q[:, j * HD:(j + 1) * HD] for j in heads], axis=0)
        run_max = jnp.full((rows, BLK), -jnp.inf, jnp.float32)
        for s in range(LIST):
            key = k_ref[0, slot_ref[local, s]]
            sc = lax.dot_general(
                stacked, key, (((1,), (1,)), ((), ())), preferred_element_type=jnp.float32
            ) + bias_sc[diag_ref[local, s]]
            score_sc[half, s] = sc
            run_max = jnp.maximum(run_max, sc)
        row_max = jnp.max(run_max, axis=1, keepdims=True)
        total = jnp.zeros((rows, BLK), jnp.float32)
        acc = jnp.zeros((rows, HD), jnp.float32)
        for s in range(LIST):
            powers = jnp.exp2((score_sc[half, s] - row_max) * exp2_scale)
            total = total + powers
            value = v_ref[0, slot_ref[local, s]]
            acc = acc + jnp.dot(
                powers.astype(jnp.bfloat16), value, preferred_element_type=jnp.float32
            )
        denominator = jnp.sum(total, axis=1, keepdims=True)
        result = (acc / denominator).astype(jnp.bfloat16)
        for k, j in enumerate(heads):
            o_ref[:, j * HD:(j + 1) * HD] = result[k * BLK:(k + 1) * BLK]


def attend(slots, diag, queries, kv_buffer):
    blocks_here = queries.shape[0] // BLK
    buffer_blocks = kv_buffer.shape[1]
    flops = 4 * blocks_here * H * BLK * LIST * BLK * HD
    grid_spec = pltpu.PrefetchScalarGridSpec(
        num_scalar_prefetch=2,
        grid=(KVH, blocks_here),
        in_specs=[
            pl.BlockSpec((BLK, GROUP * HD), lambda g, b, *_: (b, g)),
            pl.BlockSpec((1, buffer_blocks, BLK, HD), lambda g, b, *_: (0, 0, 0, g)),
            pl.BlockSpec((1, buffer_blocks, BLK, HD), lambda g, b, *_: (1, 0, 0, g)),
        ],
        out_specs=pl.BlockSpec((BLK, GROUP * HD), lambda g, b, *_: (b, g)),
        scratch_shapes=[
            pltpu.VMEM((GROUP // PAIR, LIST, PAIR * BLK, BLK), jnp.float32),
            pltpu.VMEM((2, PAIR * BLK, BLK), jnp.float32),
        ],
    )
    return pl.pallas_call(
        attend_kernel,
        out_shape=jax.ShapeDtypeStruct(queries.shape, jnp.bfloat16),
        grid_spec=grid_spec,
        compiler_params=pltpu.CompilerParams(
            dimension_semantics=("arbitrary", "arbitrary"),
            vmem_limit_bytes=24 * 1024 * 1024,
        ),
        cost_estimate=pl.CostEstimate(
            flops=flops,
            transcendentals=blocks_here * H * BLK * LIST * BLK,
            bytes_accessed=2 * queries.size * 2 + kv_buffer.size * 2,
        ),
    )(slots, diag, queries, kv_buffer, kv_buffer)


def per_device(queries, key_rows, value_rows, pattern):
    tok_rows = queries.shape[0]
    blocks_here = tok_rows // BLK
    ctx_count = lax.axis_size("ctx")
    own_index = lax.axis_index("ctx")
    kv = jnp.stack([key_rows, value_rows])
    assert blocks_here == 2 and ctx_count % 4 == 0
    early = window_blocks(kv, "ctx")
    columns = blocks_here * ctx_count // STRIDE
    spread = STRIDE // blocks_here
    column_blocks = [
        tree_broadcast(kv[:, :BLK], "ctx", column * spread, ctx_count)
        for column in range(columns)
    ]
    buffer_blocks = columns + 4 * blocks_here + blocks_here
    kv_buffer = jnp.concatenate(column_blocks + early + [kv], axis=1).reshape(
        2, buffer_blocks, BLK, kv.shape[2]
    )
    first_block = own_index * blocks_here - 4 * blocks_here
    rows_pattern = lax.dynamic_slice_in_dim(pattern, own_index * blocks_here, blocks_here, 0)
    slots = jnp.where(
        rows_pattern >= first_block,
        columns + rows_pattern - first_block,
        rows_pattern // STRIDE,
    )
    slots = jnp.clip(slots, 0, buffer_blocks - 1).astype(jnp.int32)
    blocks = own_index * blocks_here + jnp.arange(blocks_here, dtype=jnp.int32)
    diag = (rows_pattern == blocks[:, None]).astype(jnp.int32)
    return attend(slots, diag, queries, kv_buffer)


def solution(mesh):
    placed = (
        P(("groups", "ctx"), None),
        P(("groups", "ctx"), None),
        P(("groups", "ctx"), None),
        P(),
    )
    return jax.shard_map(
        per_device,
        mesh=mesh,
        in_specs=placed,
        out_specs=P(("groups", "ctx"), None),
        check_vma=False,
    )
```

```python
import functools

import jax
import jax.numpy as jnp
from jax import lax
from jax.experimental import pallas as pl
from jax.experimental.pallas import tpu as pltpu
from jax.sharding import PartitionSpec as P

H = 32
KVH = 8
HD = 128
BLK = 128
WIN = 8
STRIDE = 32
LIST = 11
GROUP = H // KVH
PAIR = 2


def shifted(shard, axis, by, sends):
    size = lax.axis_size(axis)
    pairs = [(i, i + by) for i in range(size) if sends(i) and 0 <= i + by < size]
    return lax.ppermute(shard, axis, pairs)


def window_blocks(kv, axis):
    index = lax.axis_index(axis)
    y_low = (index // 2) % 2 == 0
    core0 = index % 2 == 0
    back4 = shifted(kv, axis, 4, lambda i: True)
    up_y = shifted(kv, axis, 2, lambda i: (i // 2) % 2 == 0)
    next_core = shifted(kv, axis, 1, lambda i: i % 2 == 0)
    down_y = shifted(back4, axis, -2, lambda i: (i // 2) % 2 == 1)
    back2 = jnp.where(y_low, down_y, up_y)
    partner_back4 = shifted(back4, axis, -1, lambda i: i % 2 == 1)
    size = lax.axis_size(axis)
    swap_pairs = [(i, i ^ 1) for i in range(size)]
    partner_back2 = lax.ppermute(back2, axis, swap_pairs)
    back3 = jnp.where(core0, partner_back4, partner_back2)
    back1 = jnp.where(core0, partner_back2, next_core)
    return [back4, back3, back2, back1]


def tree_broadcast(block, axis, source, size):
    index = lax.axis_index(axis)
    span = size - source
    held = block
    dist = 1
    while dist < span:
        dist *= 2
    dist //= 2
    while dist >= 1:
        pairs = [
            (source + j, source + j + dist)
            for j in range(0, span, 2 * dist)
            if j + dist < span
        ]
        got = lax.ppermute(held, axis, pairs)
        rel = index - source
        takes = (rel >= 0) & (rel % (2 * dist) == dist)
        held = jnp.where(takes, got, held)
        dist //= 2
    return held


def attend_kernel(slot_ref, diag_ref, q_ref, k_ref, v_ref, o_ref, score_sc, bias_sc):
    local = pl.program_id(1)
    exp2_scale = (HD ** (-0.5)) * 1.4426950408889634
    rows = PAIR * BLK
    row = lax.broadcasted_iota(jnp.int32, (rows, BLK), 0) % BLK
    col = lax.broadcasted_iota(jnp.int32, (rows, BLK), 1)
    bias_sc[0] = jnp.zeros((rows, BLK), jnp.float32)
    bias_sc[1] = jnp.where(col > row, -jnp.inf, 0.0).astype(jnp.float32)
    q = q_ref[...]
    for half in range(GROUP // PAIR):
        heads = range(half * PAIR, (half + 1) * PAIR)
        stacked = jnp.concatenate([q[:, j * HD:(j + 1) * HD] for j in heads], axis=0)
        run_max = jnp.full((rows, BLK), -jnp.inf, jnp.float32)
        for s in range(LIST):
            key_t = k_ref[0, slot_ref[local, s], 0]
            sc = jnp.dot(
                stacked, key_t, preferred_element_type=jnp.float32
            ) + bias_sc[diag_ref[local, s]]
            score_sc[half, s] = sc
            run_max = jnp.maximum(run_max, sc)
        row_max = jnp.max(run_max, axis=1, keepdims=True)
        total = jnp.zeros((rows, BLK), jnp.float32)
        acc = jnp.zeros((rows, HD), jnp.float32)
        for s in range(LIST):
            powers = jnp.exp2((score_sc[half, s] - row_max) * exp2_scale)
            total = total + powers
            value = v_ref[0, slot_ref[local, s], 0]
            acc = acc + jnp.dot(
                powers.astype(jnp.bfloat16), value, preferred_element_type=jnp.float32
            )
        denominator = jnp.sum(total, axis=1, keepdims=True)
        result = (acc / denominator).astype(jnp.bfloat16)
        for k, j in enumerate(heads):
            o_ref[:, j * HD:(j + 1) * HD] = result[k * BLK:(k + 1) * BLK]


def attend(slots, diag, queries, kv_buffer):
    blocks_here = queries.shape[0] // BLK
    buffer_blocks = kv_buffer.shape[1]
    flops = 4 * blocks_here * H * BLK * LIST * BLK * HD
    grid_spec = pltpu.PrefetchScalarGridSpec(
        num_scalar_prefetch=2,
        grid=(KVH, blocks_here),
        in_specs=[
            pl.BlockSpec((BLK, GROUP * HD), lambda g, b, *_: (b, g)),
            pl.BlockSpec((1, buffer_blocks, 1, HD, BLK), lambda g, b, *_: (0, 0, g, 0, 0)),
            pl.BlockSpec((1, buffer_blocks, 1, BLK, HD), lambda g, b, *_: (1, 0, g, 0, 0)),
        ],
        out_specs=pl.BlockSpec((BLK, GROUP * HD), lambda g, b, *_: (b, g)),
        scratch_shapes=[
            pltpu.VMEM((GROUP // PAIR, LIST, PAIR * BLK, BLK), jnp.float32),
            pltpu.VMEM((2, PAIR * BLK, BLK), jnp.float32),
        ],
    )
    return pl.pallas_call(
        attend_kernel,
        out_shape=jax.ShapeDtypeStruct(queries.shape, jnp.bfloat16),
        grid_spec=grid_spec,
        compiler_params=pltpu.CompilerParams(
            dimension_semantics=("arbitrary", "arbitrary"),
            vmem_limit_bytes=24 * 1024 * 1024,
        ),
        cost_estimate=pl.CostEstimate(
            flops=flops,
            transcendentals=blocks_here * H * BLK * LIST * BLK,
            bytes_accessed=2 * queries.size * 2 + kv_buffer.size * 2,
        ),
    )(slots, diag, queries, kv_buffer, kv_buffer)


def per_device(queries, key_rows, value_rows, pattern):
    tok_rows = queries.shape[0]
    blocks_here = tok_rows // BLK
    ctx_count = lax.axis_size("ctx")
    own_index = lax.axis_index("ctx")
    key_tiles = key_rows.reshape(blocks_here, BLK, KVH, HD).transpose(0, 2, 3, 1)
    value_tiles = value_rows.reshape(blocks_here, BLK, KVH, HD).transpose(0, 2, 1, 3)
    kv = jnp.stack([key_tiles, value_tiles])
    assert blocks_here == 2 and ctx_count % 4 == 0
    early = window_blocks(kv, "ctx")
    columns = blocks_here * ctx_count // STRIDE
    spread = STRIDE // blocks_here
    column_blocks = [
        tree_broadcast(kv[:, :1], "ctx", column * spread, ctx_count)
        for column in range(columns)
    ]
    buffer_blocks = columns + 4 * blocks_here + blocks_here
    kv_buffer = jnp.concatenate(column_blocks + early + [kv], axis=1)
    first_block = own_index * blocks_here - 4 * blocks_here
    rows_pattern = lax.dynamic_slice_in_dim(pattern, own_index * blocks_here, blocks_here, 0)
    slots = jnp.where(
        rows_pattern >= first_block,
        columns + rows_pattern - first_block,
        rows_pattern // STRIDE,
    )
    slots = jnp.clip(slots, 0, buffer_blocks - 1).astype(jnp.int32)
    blocks = own_index * blocks_here + jnp.arange(blocks_here, dtype=jnp.int32)
    diag = (rows_pattern == blocks[:, None]).astype(jnp.int32)
    return attend(slots, diag, queries, kv_buffer)


def solution(mesh):
    placed = (
        P(("groups", "ctx"), None),
        P(("groups", "ctx"), None),
        P(("groups", "ctx"), None),
        P(),
    )
    return jax.shard_map(
        per_device,
        mesh=mesh,
        in_specs=placed,
        out_specs=P(("groups", "ctx"), None),
        check_vma=False,
    )
```

```python
import functools

import jax
import jax.numpy as jnp
from jax import lax
from jax.experimental import pallas as pl
from jax.experimental.pallas import tpu as pltpu
from jax.sharding import PartitionSpec as P

H = 32
KVH = 8
HD = 128
BLK = 128
WIN = 8
STRIDE = 32
LIST = 11
GROUP = H // KVH
PAIR = 2
KV_STEP = 2


def shifted(shard, axis, by, sends):
    size = lax.axis_size(axis)
    pairs = [(i, i + by) for i in range(size) if sends(i) and 0 <= i + by < size]
    return lax.ppermute(shard, axis, pairs)


def window_blocks(kv, axis):
    index = lax.axis_index(axis)
    y_low = (index // 2) % 2 == 0
    core0 = index % 2 == 0
    back4 = shifted(kv, axis, 4, lambda i: True)
    up_y = shifted(kv, axis, 2, lambda i: (i // 2) % 2 == 0)
    next_core = shifted(kv, axis, 1, lambda i: i % 2 == 0)
    down_y = shifted(back4, axis, -2, lambda i: (i // 2) % 2 == 1)
    back2 = jnp.where(y_low, down_y, up_y)
    partner_back4 = shifted(back4, axis, -1, lambda i: i % 2 == 1)
    size = lax.axis_size(axis)
    swap_pairs = [(i, i ^ 1) for i in range(size)]
    partner_back2 = lax.ppermute(back2, axis, swap_pairs)
    back3 = jnp.where(core0, partner_back4, partner_back2)
    back1 = jnp.where(core0, partner_back2, next_core)
    return [back4, back3, back2, back1]


def tree_broadcast(block, axis, source, size):
    index = lax.axis_index(axis)
    span = size - source
    held = block
    dist = 1
    while dist < span:
        dist *= 2
    dist //= 2
    while dist >= 1:
        pairs = [
            (source + j, source + j + dist)
            for j in range(0, span, 2 * dist)
            if j + dist < span
        ]
        got = lax.ppermute(held, axis, pairs)
        rel = index - source
        takes = (rel >= 0) & (rel % (2 * dist) == dist)
        held = jnp.where(takes, got, held)
        dist //= 2
    return held


def attend_kernel(slot_ref, diag_ref, q_ref, k_ref, v_ref, o_ref, score_sc, bias_sc):
    local = pl.program_id(1)
    exp2_scale = (HD ** (-0.5)) * 1.4426950408889634
    rows = PAIR * BLK
    row = lax.broadcasted_iota(jnp.int32, (rows, BLK), 0) % BLK
    col = lax.broadcasted_iota(jnp.int32, (rows, BLK), 1)
    bias_sc[0] = jnp.zeros((rows, BLK), jnp.float32)
    bias_sc[1] = jnp.where(col > row, -jnp.inf, 0.0).astype(jnp.float32)
    q = q_ref[...]
    chain = 0
    for kv_head in range(KV_STEP):
        kv_lanes = slice(kv_head * HD, (kv_head + 1) * HD)
        for half in range(GROUP // PAIR):
            heads = [kv_head * GROUP + j for j in range(half * PAIR, (half + 1) * PAIR)]
            stacked = jnp.concatenate([q[:, j * HD:(j + 1) * HD] for j in heads], axis=0)
            run_max = jnp.full((rows, BLK), -jnp.inf, jnp.float32)
            for s in range(LIST):
                key = k_ref[0, slot_ref[local, s], :, kv_lanes]
                sc = lax.dot_general(
                    stacked, key, (((1,), (1,)), ((), ())), preferred_element_type=jnp.float32
                ) + bias_sc[diag_ref[local, s]]
                score_sc[chain, s] = sc
                run_max = jnp.maximum(run_max, sc)
            row_max = jnp.max(run_max, axis=1, keepdims=True)
            total = jnp.zeros((rows, BLK), jnp.float32)
            acc = jnp.zeros((rows, HD), jnp.float32)
            for s in range(LIST):
                powers = jnp.exp2((score_sc[chain, s] - row_max) * exp2_scale)
                total = total + powers
                value = v_ref[0, slot_ref[local, s], :, kv_lanes]
                acc = acc + jnp.dot(
                    powers.astype(jnp.bfloat16), value, preferred_element_type=jnp.float32
                )
            denominator = jnp.sum(total, axis=1, keepdims=True)
            result = (acc / denominator).astype(jnp.bfloat16)
            for k, j in enumerate(heads):
                o_ref[:, j * HD:(j + 1) * HD] = result[k * BLK:(k + 1) * BLK]
            chain += 1


def attend(slots, diag, queries, kv_buffer):
    blocks_here = queries.shape[0] // BLK
    buffer_blocks = kv_buffer.shape[1]
    flops = 4 * blocks_here * H * BLK * LIST * BLK * HD
    grid_spec = pltpu.PrefetchScalarGridSpec(
        num_scalar_prefetch=2,
        grid=(KVH // KV_STEP, blocks_here),
        in_specs=[
            pl.BlockSpec((BLK, KV_STEP * GROUP * HD), lambda g, b, *_: (b, g)),
            pl.BlockSpec((1, buffer_blocks, BLK, KV_STEP * HD), lambda g, b, *_: (0, 0, 0, g)),
            pl.BlockSpec((1, buffer_blocks, BLK, KV_STEP * HD), lambda g, b, *_: (1, 0, 0, g)),
        ],
        out_specs=pl.BlockSpec((BLK, KV_STEP * GROUP * HD), lambda g, b, *_: (b, g)),
        scratch_shapes=[
            pltpu.VMEM((KV_STEP * GROUP // PAIR, LIST, PAIR * BLK, BLK), jnp.float32),
            pltpu.VMEM((2, PAIR * BLK, BLK), jnp.float32),
        ],
    )
    return pl.pallas_call(
        attend_kernel,
        out_shape=jax.ShapeDtypeStruct(queries.shape, jnp.bfloat16),
        grid_spec=grid_spec,
        compiler_params=pltpu.CompilerParams(
            dimension_semantics=("arbitrary", "arbitrary"),
            vmem_limit_bytes=24 * 1024 * 1024,
        ),
        cost_estimate=pl.CostEstimate(
            flops=flops,
            transcendentals=blocks_here * H * BLK * LIST * BLK,
            bytes_accessed=2 * queries.size * 2 + kv_buffer.size * 2,
        ),
    )(slots, diag, queries, kv_buffer, kv_buffer)


def per_device(queries, key_rows, value_rows, pattern):
    tok_rows = queries.shape[0]
    blocks_here = tok_rows // BLK
    ctx_count = lax.axis_size("ctx")
    own_index = lax.axis_index("ctx")
    kv = jnp.stack([key_rows, value_rows])
    assert blocks_here == 2 and ctx_count % 4 == 0
    early = window_blocks(kv, "ctx")
    columns = blocks_here * ctx_count // STRIDE
    spread = STRIDE // blocks_here
    column_blocks = [
        tree_broadcast(kv[:, :BLK], "ctx", column * spread, ctx_count)
        for column in range(columns)
    ]
    buffer_blocks = columns + 4 * blocks_here + blocks_here
    kv_buffer = jnp.concatenate(column_blocks + early + [kv], axis=1).reshape(
        2, buffer_blocks, BLK, kv.shape[2]
    )
    first_block = own_index * blocks_here - 4 * blocks_here
    rows_pattern = lax.dynamic_slice_in_dim(pattern, own_index * blocks_here, blocks_here, 0)
    slots = jnp.where(
        rows_pattern >= first_block,
        columns + rows_pattern - first_block,
        rows_pattern // STRIDE,
    )
    slots = jnp.clip(slots, 0, buffer_blocks - 1).astype(jnp.int32)
    blocks = own_index * blocks_here + jnp.arange(blocks_here, dtype=jnp.int32)
    diag = (rows_pattern == blocks[:, None]).astype(jnp.int32)
    return attend(slots, diag, queries, kv_buffer)


def solution(mesh):
    placed = (
        P(("groups", "ctx"), None),
        P(("groups", "ctx"), None),
        P(("groups", "ctx"), None),
        P(),
    )
    return jax.shard_map(
        per_device,
        mesh=mesh,
        in_specs=placed,
        out_specs=P(("groups", "ctx"), None),
        check_vma=False,
    )
```

```python
import functools

import jax
import jax.numpy as jnp
from jax import lax
from jax.experimental import pallas as pl
from jax.experimental.pallas import tpu as pltpu
from jax.sharding import PartitionSpec as P

H = 32
KVH = 8
HD = 128
BLK = 128
WIN = 8
STRIDE = 32
LIST = 11
GROUP = H // KVH
PAIR = 2
KV_STEP = 4


def shifted(shard, axis, by, sends):
    size = lax.axis_size(axis)
    pairs = [(i, i + by) for i in range(size) if sends(i) and 0 <= i + by < size]
    return lax.ppermute(shard, axis, pairs)


def window_blocks(kv, axis):
    index = lax.axis_index(axis)
    y_low = (index // 2) % 2 == 0
    core0 = index % 2 == 0
    back4 = shifted(kv, axis, 4, lambda i: True)
    up_y = shifted(kv, axis, 2, lambda i: (i // 2) % 2 == 0)
    next_core = shifted(kv, axis, 1, lambda i: i % 2 == 0)
    down_y = shifted(back4, axis, -2, lambda i: (i // 2) % 2 == 1)
    back2 = jnp.where(y_low, down_y, up_y)
    partner_back4 = shifted(back4, axis, -1, lambda i: i % 2 == 1)
    size = lax.axis_size(axis)
    swap_pairs = [(i, i ^ 1) for i in range(size)]
    partner_back2 = lax.ppermute(back2, axis, swap_pairs)
    back3 = jnp.where(core0, partner_back4, partner_back2)
    back1 = jnp.where(core0, partner_back2, next_core)
    return [back4, back3, back2, back1]


def tree_broadcast(block, axis, source, size):
    index = lax.axis_index(axis)
    span = size - source
    held = block
    dist = 1
    while dist < span:
        dist *= 2
    dist //= 2
    while dist >= 1:
        pairs = [
            (source + j, source + j + dist)
            for j in range(0, span, 2 * dist)
            if j + dist < span
        ]
        got = lax.ppermute(held, axis, pairs)
        rel = index - source
        takes = (rel >= 0) & (rel % (2 * dist) == dist)
        held = jnp.where(takes, got, held)
        dist //= 2
    return held


def attend_kernel(slot_ref, diag_ref, q_ref, k_ref, v_ref, o_ref, score_sc, bias_sc):
    local = pl.program_id(1)
    exp2_scale = (HD ** (-0.5)) * 1.4426950408889634
    rows = PAIR * BLK
    row = lax.broadcasted_iota(jnp.int32, (rows, BLK), 0) % BLK
    col = lax.broadcasted_iota(jnp.int32, (rows, BLK), 1)
    bias_sc[0] = jnp.zeros((rows, BLK), jnp.float32)
    bias_sc[1] = jnp.where(col > row, -jnp.inf, 0.0).astype(jnp.float32)
    q = q_ref[...]
    chain = 0
    for kv_head in range(KV_STEP):
        kv_lanes = slice(kv_head * HD, (kv_head + 1) * HD)
        for half in range(GROUP // PAIR):
            heads = [kv_head * GROUP + j for j in range(half * PAIR, (half + 1) * PAIR)]
            stacked = jnp.concatenate([q[:, j * HD:(j + 1) * HD] for j in heads], axis=0)
            run_max = jnp.full((rows, BLK), -jnp.inf, jnp.float32)
            for s in range(LIST):
                key = k_ref[0, slot_ref[local, s], :, kv_lanes]
                sc = lax.dot_general(
                    stacked, key, (((1,), (1,)), ((), ())), preferred_element_type=jnp.float32
                ) + bias_sc[diag_ref[local, s]]
                score_sc[chain, s] = sc
                run_max = jnp.maximum(run_max, sc)
            row_max = jnp.max(run_max, axis=1, keepdims=True)
            total = jnp.zeros((rows, BLK), jnp.float32)
            acc = jnp.zeros((rows, HD), jnp.float32)
            for s in range(LIST):
                powers = jnp.exp2((score_sc[chain, s] - row_max) * exp2_scale)
                total = total + powers
                value = v_ref[0, slot_ref[local, s], :, kv_lanes]
                acc = acc + jnp.dot(
                    powers.astype(jnp.bfloat16), value, preferred_element_type=jnp.float32
                )
            denominator = jnp.sum(total, axis=1, keepdims=True)
            result = (acc / denominator).astype(jnp.bfloat16)
            for k, j in enumerate(heads):
                o_ref[:, j * HD:(j + 1) * HD] = result[k * BLK:(k + 1) * BLK]
            chain += 1


def attend(slots, diag, queries, kv_buffer):
    blocks_here = queries.shape[0] // BLK
    buffer_blocks = kv_buffer.shape[1]
    flops = 4 * blocks_here * H * BLK * LIST * BLK * HD
    grid_spec = pltpu.PrefetchScalarGridSpec(
        num_scalar_prefetch=2,
        grid=(KVH // KV_STEP, blocks_here),
        in_specs=[
            pl.BlockSpec((BLK, KV_STEP * GROUP * HD), lambda g, b, *_: (b, g)),
            pl.BlockSpec((1, buffer_blocks, BLK, KV_STEP * HD), lambda g, b, *_: (0, 0, 0, g)),
            pl.BlockSpec((1, buffer_blocks, BLK, KV_STEP * HD), lambda g, b, *_: (1, 0, 0, g)),
        ],
        out_specs=pl.BlockSpec((BLK, KV_STEP * GROUP * HD), lambda g, b, *_: (b, g)),
        scratch_shapes=[
            pltpu.VMEM((KV_STEP * GROUP // PAIR, LIST, PAIR * BLK, BLK), jnp.float32),
            pltpu.VMEM((2, PAIR * BLK, BLK), jnp.float32),
        ],
    )
    return pl.pallas_call(
        attend_kernel,
        out_shape=jax.ShapeDtypeStruct(queries.shape, jnp.bfloat16),
        grid_spec=grid_spec,
        compiler_params=pltpu.CompilerParams(
            dimension_semantics=("arbitrary", "arbitrary"),
            vmem_limit_bytes=40 * 1024 * 1024,
        ),
        cost_estimate=pl.CostEstimate(
            flops=flops,
            transcendentals=blocks_here * H * BLK * LIST * BLK,
            bytes_accessed=2 * queries.size * 2 + kv_buffer.size * 2,
        ),
    )(slots, diag, queries, kv_buffer, kv_buffer)


def per_device(queries, key_rows, value_rows, pattern):
    tok_rows = queries.shape[0]
    blocks_here = tok_rows // BLK
    ctx_count = lax.axis_size("ctx")
    own_index = lax.axis_index("ctx")
    kv = jnp.stack([key_rows, value_rows])
    assert blocks_here == 2 and ctx_count % 4 == 0
    early = window_blocks(kv, "ctx")
    columns = blocks_here * ctx_count // STRIDE
    spread = STRIDE // blocks_here
    column_blocks = [
        tree_broadcast(kv[:, :BLK], "ctx", column * spread, ctx_count)
        for column in range(columns)
    ]
    buffer_blocks = columns + 4 * blocks_here + blocks_here
    kv_buffer = jnp.concatenate(column_blocks + early + [kv], axis=1).reshape(
        2, buffer_blocks, BLK, kv.shape[2]
    )
    first_block = own_index * blocks_here - 4 * blocks_here
    rows_pattern = lax.dynamic_slice_in_dim(pattern, own_index * blocks_here, blocks_here, 0)
    slots = jnp.where(
        rows_pattern >= first_block,
        columns + rows_pattern - first_block,
        rows_pattern // STRIDE,
    )
    slots = jnp.clip(slots, 0, buffer_blocks - 1).astype(jnp.int32)
    blocks = own_index * blocks_here + jnp.arange(blocks_here, dtype=jnp.int32)
    diag = (rows_pattern == blocks[:, None]).astype(jnp.int32)
    return attend(slots, diag, queries, kv_buffer)


def solution(mesh):
    placed = (
        P(("groups", "ctx"), None),
        P(("groups", "ctx"), None),
        P(("groups", "ctx"), None),
        P(),
    )
    return jax.shard_map(
        per_device,
        mesh=mesh,
        in_specs=placed,
        out_specs=P(("groups", "ctx"), None),
        check_vma=False,
    )
```

```python
import functools

import jax
import jax.numpy as jnp
from jax import lax
from jax.experimental import pallas as pl
from jax.experimental.pallas import tpu as pltpu
from jax.sharding import PartitionSpec as P

H = 32
KVH = 8
HD = 128
BLK = 128
WIN = 8
STRIDE = 32
LIST = 11
GROUP = H // KVH
PAIR = 2
KV_STEP = 4


def shifted(shard, axis, by, sends):
    size = lax.axis_size(axis)
    pairs = [(i, i + by) for i in range(size) if sends(i) and 0 <= i + by < size]
    return lax.ppermute(shard, axis, pairs)


def window_blocks(kv, axis):
    index = lax.axis_index(axis)
    y_low = (index // 2) % 2 == 0
    core0 = index % 2 == 0
    back4 = shifted(kv, axis, 4, lambda i: True)
    up_y = shifted(kv, axis, 2, lambda i: (i // 2) % 2 == 0)
    next_core = shifted(kv, axis, 1, lambda i: i % 2 == 0)
    down_y = shifted(back4, axis, -2, lambda i: (i // 2) % 2 == 1)
    back2 = jnp.where(y_low, down_y, up_y)
    partner_back4 = shifted(back4, axis, -1, lambda i: i % 2 == 1)
    size = lax.axis_size(axis)
    swap_pairs = [(i, i ^ 1) for i in range(size)]
    partner_back2 = lax.ppermute(back2, axis, swap_pairs)
    back3 = jnp.where(core0, partner_back4, partner_back2)
    back1 = jnp.where(core0, partner_back2, next_core)
    return [back4, back3, back2, back1]


def tree_broadcast(block, axis, source, size):
    index = lax.axis_index(axis)
    span = size - source
    held = block
    dist = 1
    while dist < span:
        dist *= 2
    dist //= 2
    while dist >= 1:
        pairs = [
            (source + j, source + j + dist)
            for j in range(0, span, 2 * dist)
            if j + dist < span
        ]
        got = lax.ppermute(held, axis, pairs)
        rel = index - source
        takes = (rel >= 0) & (rel % (2 * dist) == dist)
        held = jnp.where(takes, got, held)
        dist //= 2
    return held


def attend_kernel(slot_ref, diag_ref, q_ref, k_ref, v_ref, o_ref, score_sc, bias_sc):
    local = pl.program_id(1)
    exp2_scale = (HD ** (-0.5)) * 1.4426950408889634
    rows = PAIR * BLK
    row = lax.broadcasted_iota(jnp.int32, (rows, BLK), 0) % BLK
    col = lax.broadcasted_iota(jnp.int32, (rows, BLK), 1)
    bias_sc[0] = jnp.zeros((rows, BLK), jnp.float32)
    bias_sc[1] = jnp.where(col > row, -jnp.inf, 0.0).astype(jnp.float32)
    q = q_ref[...]
    chains = []
    for kv_head in range(KV_STEP):
        for half in range(GROUP // PAIR):
            heads = [kv_head * GROUP + j for j in range(half * PAIR, (half + 1) * PAIR)]
            chains.append((slice(kv_head * HD, (kv_head + 1) * HD), heads))
    row_maxes = []
    for chain, (kv_lanes, heads) in enumerate(chains):
        stacked = jnp.concatenate([q[:, j * HD:(j + 1) * HD] for j in heads], axis=0)
        run_max = jnp.full((rows, BLK), -jnp.inf, jnp.float32)
        for s in range(LIST):
            key = k_ref[0, slot_ref[local, s], :, kv_lanes]
            sc = lax.dot_general(
                stacked, key, (((1,), (1,)), ((), ())), preferred_element_type=jnp.float32
            ) + bias_sc[diag_ref[local, s]]
            score_sc[chain, s] = sc
            run_max = jnp.maximum(run_max, sc)
        row_maxes.append(jnp.max(run_max, axis=1, keepdims=True))
    for chain, (kv_lanes, heads) in enumerate(chains):
        total = jnp.zeros((rows, BLK), jnp.float32)
        acc = jnp.zeros((rows, HD), jnp.float32)
        for s in range(LIST):
            powers = jnp.exp2((score_sc[chain, s] - row_maxes[chain]) * exp2_scale)
            total = total + powers
            value = v_ref[0, slot_ref[local, s], :, kv_lanes]
            acc = acc + jnp.dot(
                powers.astype(jnp.bfloat16), value, preferred_element_type=jnp.float32
            )
        denominator = jnp.sum(total, axis=1, keepdims=True)
        result = (acc / denominator).astype(jnp.bfloat16)
        for k, j in enumerate(heads):
            o_ref[:, j * HD:(j + 1) * HD] = result[k * BLK:(k + 1) * BLK]


def attend(slots, diag, queries, kv_buffer):
    blocks_here = queries.shape[0] // BLK
    buffer_blocks = kv_buffer.shape[1]
    flops = 4 * blocks_here * H * BLK * LIST * BLK * HD
    grid_spec = pltpu.PrefetchScalarGridSpec(
        num_scalar_prefetch=2,
        grid=(KVH // KV_STEP, blocks_here),
        in_specs=[
            pl.BlockSpec((BLK, KV_STEP * GROUP * HD), lambda g, b, *_: (b, g)),
            pl.BlockSpec((1, buffer_blocks, BLK, KV_STEP * HD), lambda g, b, *_: (0, 0, 0, g)),
            pl.BlockSpec((1, buffer_blocks, BLK, KV_STEP * HD), lambda g, b, *_: (1, 0, 0, g)),
        ],
        out_specs=pl.BlockSpec((BLK, KV_STEP * GROUP * HD), lambda g, b, *_: (b, g)),
        scratch_shapes=[
            pltpu.VMEM((KV_STEP * GROUP // PAIR, LIST, PAIR * BLK, BLK), jnp.float32),
            pltpu.VMEM((2, PAIR * BLK, BLK), jnp.float32),
        ],
    )
    return pl.pallas_call(
        attend_kernel,
        out_shape=jax.ShapeDtypeStruct(queries.shape, jnp.bfloat16),
        grid_spec=grid_spec,
        compiler_params=pltpu.CompilerParams(
            dimension_semantics=("arbitrary", "arbitrary"),
            vmem_limit_bytes=40 * 1024 * 1024,
        ),
        cost_estimate=pl.CostEstimate(
            flops=flops,
            transcendentals=blocks_here * H * BLK * LIST * BLK,
            bytes_accessed=2 * queries.size * 2 + kv_buffer.size * 2,
        ),
    )(slots, diag, queries, kv_buffer, kv_buffer)


def per_device(queries, key_rows, value_rows, pattern):
    tok_rows = queries.shape[0]
    blocks_here = tok_rows // BLK
    ctx_count = lax.axis_size("ctx")
    own_index = lax.axis_index("ctx")
    kv = jnp.stack([key_rows, value_rows])
    assert blocks_here == 2 and ctx_count % 4 == 0
    early = window_blocks(kv, "ctx")
    columns = blocks_here * ctx_count // STRIDE
    spread = STRIDE // blocks_here
    column_blocks = [
        tree_broadcast(kv[:, :BLK], "ctx", column * spread, ctx_count)
        for column in range(columns)
    ]
    buffer_blocks = columns + 4 * blocks_here + blocks_here
    kv_buffer = jnp.concatenate(column_blocks + early + [kv], axis=1).reshape(
        2, buffer_blocks, BLK, kv.shape[2]
    )
    first_block = own_index * blocks_here - 4 * blocks_here
    rows_pattern = lax.dynamic_slice_in_dim(pattern, own_index * blocks_here, blocks_here, 0)
    slots = jnp.where(
        rows_pattern >= first_block,
        columns + rows_pattern - first_block,
        rows_pattern // STRIDE,
    )
    slots = jnp.clip(slots, 0, buffer_blocks - 1).astype(jnp.int32)
    blocks = own_index * blocks_here + jnp.arange(blocks_here, dtype=jnp.int32)
    diag = (rows_pattern == blocks[:, None]).astype(jnp.int32)
    return attend(slots, diag, queries, kv_buffer)


def solution(mesh):
    placed = (
        P(("groups", "ctx"), None),
        P(("groups", "ctx"), None),
        P(("groups", "ctx"), None),
        P(),
    )
    return jax.shard_map(
        per_device,
        mesh=mesh,
        in_specs=placed,
        out_specs=P(("groups", "ctx"), None),
        check_vma=False,
    )
```

```python
import functools

import jax
import jax.numpy as jnp
from jax import lax
from jax.experimental import pallas as pl
from jax.experimental.pallas import tpu as pltpu
from jax.sharding import PartitionSpec as P

H = 32
KVH = 8
HD = 128
BLK = 128
WIN = 8
STRIDE = 32
LIST = 11
GROUP = H // KVH
PAIR = 2
KV_STEP = 8
SLOTS = 8


def shifted(shard, axis, by, sends):
    size = lax.axis_size(axis)
    pairs = [(i, i + by) for i in range(size) if sends(i) and 0 <= i + by < size]
    return lax.ppermute(shard, axis, pairs)


def window_blocks(kv, axis):
    index = lax.axis_index(axis)
    y_low = (index // 2) % 2 == 0
    core0 = index % 2 == 0
    back4 = shifted(kv, axis, 4, lambda i: True)
    up_y = shifted(kv, axis, 2, lambda i: (i // 2) % 2 == 0)
    next_core = shifted(kv, axis, 1, lambda i: i % 2 == 0)
    down_y = shifted(back4, axis, -2, lambda i: (i // 2) % 2 == 1)
    back2 = jnp.where(y_low, down_y, up_y)
    partner_back4 = shifted(back4, axis, -1, lambda i: i % 2 == 1)
    size = lax.axis_size(axis)
    swap_pairs = [(i, i ^ 1) for i in range(size)]
    partner_back2 = lax.ppermute(back2, axis, swap_pairs)
    back3 = jnp.where(core0, partner_back4, partner_back2)
    back1 = jnp.where(core0, partner_back2, next_core)
    return [back4, back3, back2, back1]


def tree_broadcast(block, axis, source, size):
    index = lax.axis_index(axis)
    span = size - source
    held = block
    dist = 1
    while dist < span:
        dist *= 2
    dist //= 2
    while dist >= 1:
        pairs = [
            (source + j, source + j + dist)
            for j in range(0, span, 2 * dist)
            if j + dist < span
        ]
        got = lax.ppermute(held, axis, pairs)
        rel = index - source
        takes = (rel >= 0) & (rel % (2 * dist) == dist)
        held = jnp.where(takes, got, held)
        dist //= 2
    return held


def attend_kernel(slot_ref, diag_ref, q_ref, k_ref, v_ref, o_ref, score_sc, bias_sc):
    local = pl.program_id(1)
    exp2_scale = (HD ** (-0.5)) * 1.4426950408889634
    rows = PAIR * BLK
    row = lax.broadcasted_iota(jnp.int32, (rows, BLK), 0) % BLK
    col = lax.broadcasted_iota(jnp.int32, (rows, BLK), 1)
    bias_sc[0] = jnp.zeros((rows, BLK), jnp.float32)
    bias_sc[1] = jnp.where(col > row, -jnp.inf, 0.0).astype(jnp.float32)
    q = q_ref[...]
    chain = 0
    for kv_head in range(KV_STEP):
        kv_lanes = slice(kv_head * HD, (kv_head + 1) * HD)
        for half in range(GROUP // PAIR):
            heads = [kv_head * GROUP + j for j in range(half * PAIR, (half + 1) * PAIR)]
            stacked = jnp.concatenate([q[:, j * HD:(j + 1) * HD] for j in heads], axis=0)
            run_max = jnp.full((rows, BLK), -jnp.inf, jnp.float32)
            for s in range(LIST):
                key = k_ref[0, slot_ref[local, s], :, kv_lanes]
                sc = lax.dot_general(
                    stacked, key, (((1,), (1,)), ((), ())), preferred_element_type=jnp.float32
                ) + bias_sc[diag_ref[local, s]]
                score_sc[chain % SLOTS, s] = sc
                run_max = jnp.maximum(run_max, sc)
            row_max = jnp.max(run_max, axis=1, keepdims=True)
            total = jnp.zeros((rows, BLK), jnp.float32)
            acc = jnp.zeros((rows, HD), jnp.float32)
            for s in range(LIST):
                powers = jnp.exp2((score_sc[chain % SLOTS, s] - row_max) * exp2_scale)
                total = total + powers
                value = v_ref[0, slot_ref[local, s], :, kv_lanes]
                acc = acc + jnp.dot(
                    powers.astype(jnp.bfloat16), value, preferred_element_type=jnp.float32
                )
            denominator = jnp.sum(total, axis=1, keepdims=True)
            result = (acc / denominator).astype(jnp.bfloat16)
            for k, j in enumerate(heads):
                o_ref[:, j * HD:(j + 1) * HD] = result[k * BLK:(k + 1) * BLK]
            chain += 1


def attend(slots, diag, queries, kv_buffer):
    blocks_here = queries.shape[0] // BLK
    buffer_blocks = kv_buffer.shape[1]
    flops = 4 * blocks_here * H * BLK * LIST * BLK * HD
    grid_spec = pltpu.PrefetchScalarGridSpec(
        num_scalar_prefetch=2,
        grid=(KVH // KV_STEP, blocks_here),
        in_specs=[
            pl.BlockSpec((BLK, KV_STEP * GROUP * HD), lambda g, b, *_: (b, g)),
            pl.BlockSpec((1, buffer_blocks, BLK, KV_STEP * HD), lambda g, b, *_: (0, 0, 0, g)),
            pl.BlockSpec((1, buffer_blocks, BLK, KV_STEP * HD), lambda g, b, *_: (1, 0, 0, g)),
        ],
        out_specs=pl.BlockSpec((BLK, KV_STEP * GROUP * HD), lambda g, b, *_: (b, g)),
        scratch_shapes=[
            pltpu.VMEM((SLOTS, LIST, PAIR * BLK, BLK), jnp.float32),
            pltpu.VMEM((2, PAIR * BLK, BLK), jnp.float32),
        ],
    )
    return pl.pallas_call(
        attend_kernel,
        out_shape=jax.ShapeDtypeStruct(queries.shape, jnp.bfloat16),
        grid_spec=grid_spec,
        compiler_params=pltpu.CompilerParams(
            dimension_semantics=("arbitrary", "arbitrary"),
            vmem_limit_bytes=40 * 1024 * 1024,
        ),
        cost_estimate=pl.CostEstimate(
            flops=flops,
            transcendentals=blocks_here * H * BLK * LIST * BLK,
            bytes_accessed=2 * queries.size * 2 + kv_buffer.size * 2,
        ),
    )(slots, diag, queries, kv_buffer, kv_buffer)


def per_device(queries, key_rows, value_rows, pattern):
    tok_rows = queries.shape[0]
    blocks_here = tok_rows // BLK
    ctx_count = lax.axis_size("ctx")
    own_index = lax.axis_index("ctx")
    kv = jnp.stack([key_rows, value_rows])
    assert blocks_here == 2 and ctx_count % 4 == 0
    early = window_blocks(kv, "ctx")
    columns = blocks_here * ctx_count // STRIDE
    spread = STRIDE // blocks_here
    column_blocks = [
        tree_broadcast(kv[:, :BLK], "ctx", column * spread, ctx_count)
        for column in range(columns)
    ]
    buffer_blocks = columns + 4 * blocks_here + blocks_here
    kv_buffer = jnp.concatenate(column_blocks + early + [kv], axis=1).reshape(
        2, buffer_blocks, BLK, kv.shape[2]
    )
    first_block = own_index * blocks_here - 4 * blocks_here
    rows_pattern = lax.dynamic_slice_in_dim(pattern, own_index * blocks_here, blocks_here, 0)
    slots = jnp.where(
        rows_pattern >= first_block,
        columns + rows_pattern - first_block,
        rows_pattern // STRIDE,
    )
    slots = jnp.clip(slots, 0, buffer_blocks - 1).astype(jnp.int32)
    blocks = own_index * blocks_here + jnp.arange(blocks_here, dtype=jnp.int32)
    diag = (rows_pattern == blocks[:, None]).astype(jnp.int32)
    return attend(slots, diag, queries, kv_buffer)


def solution(mesh):
    placed = (
        P(("groups", "ctx"), None),
        P(("groups", "ctx"), None),
        P(("groups", "ctx"), None),
        P(),
    )
    return jax.shard_map(
        per_device,
        mesh=mesh,
        in_specs=placed,
        out_specs=P(("groups", "ctx"), None),
        check_vma=False,
    )
```

```python
import functools

import jax
import jax.numpy as jnp
from jax import lax
from jax.experimental import pallas as pl
from jax.experimental.pallas import tpu as pltpu
from jax.sharding import PartitionSpec as P

H = 32
KVH = 8
HD = 128
BLK = 128
WIN = 8
STRIDE = 32
LIST = 11
GROUP = H // KVH
PAIR = 2
KV_STEP = 4


def shifted(shard, axis, by, sends):
    size = lax.axis_size(axis)
    pairs = [(i, i + by) for i in range(size) if sends(i) and 0 <= i + by < size]
    return lax.ppermute(shard, axis, pairs)


def window_blocks(kv, axis):
    index = lax.axis_index(axis)
    y_low = (index // 2) % 2 == 0
    core0 = index % 2 == 0
    back4 = shifted(kv, axis, 4, lambda i: True)
    up_y = shifted(kv, axis, 2, lambda i: (i // 2) % 2 == 0)
    next_core = shifted(kv, axis, 1, lambda i: i % 2 == 0)
    down_y = shifted(back4, axis, -2, lambda i: (i // 2) % 2 == 1)
    back2 = jnp.where(y_low, down_y, up_y)
    partner_back4 = shifted(back4, axis, -1, lambda i: i % 2 == 1)
    size = lax.axis_size(axis)
    swap_pairs = [(i, i ^ 1) for i in range(size)]
    partner_back2 = jnp.where(
        y_low,
        lax.ppermute(down_y, axis, swap_pairs),
        lax.ppermute(up_y, axis, swap_pairs),
    )
    back3 = jnp.where(core0, partner_back4, partner_back2)
    back1 = jnp.where(core0, partner_back2, next_core)
    return [back4, back3, back2, back1]


def tree_broadcast(block, axis, source, size):
    index = lax.axis_index(axis)
    span = size - source
    held = block
    dist = 1
    while dist < span:
        dist *= 2
    dist //= 2
    while dist >= 1:
        pairs = [
            (source + j, source + j + dist)
            for j in range(0, span, 2 * dist)
            if j + dist < span
        ]
        got = lax.ppermute(held, axis, pairs)
        rel = index - source
        takes = (rel >= 0) & (rel % (2 * dist) == dist)
        held = jnp.where(takes, got, held)
        dist //= 2
    return held


def attend_kernel(slot_ref, diag_ref, q_ref, k_ref, v_ref, o_ref, score_sc, bias_sc):
    local = pl.program_id(1)
    exp2_scale = (HD ** (-0.5)) * 1.4426950408889634
    rows = PAIR * BLK
    row = lax.broadcasted_iota(jnp.int32, (rows, BLK), 0) % BLK
    col = lax.broadcasted_iota(jnp.int32, (rows, BLK), 1)
    bias_sc[0] = jnp.zeros((rows, BLK), jnp.float32)
    bias_sc[1] = jnp.where(col > row, -jnp.inf, 0.0).astype(jnp.float32)
    q = q_ref[...]
    chain = 0
    for kv_head in range(KV_STEP):
        kv_lanes = slice(kv_head * HD, (kv_head + 1) * HD)
        for half in range(GROUP // PAIR):
            heads = [kv_head * GROUP + j for j in range(half * PAIR, (half + 1) * PAIR)]
            stacked = jnp.concatenate([q[:, j * HD:(j + 1) * HD] for j in heads], axis=0)
            run_max = jnp.full((rows, BLK), -jnp.inf, jnp.float32)
            for s in range(LIST):
                key = k_ref[0, slot_ref[local, s], :, kv_lanes]
                sc = lax.dot_general(
                    stacked, key, (((1,), (1,)), ((), ())), preferred_element_type=jnp.float32
                ) + bias_sc[diag_ref[local, s]]
                score_sc[chain, s] = sc
                run_max = jnp.maximum(run_max, sc)
            row_max = jnp.max(run_max, axis=1, keepdims=True)
            total = jnp.zeros((rows, BLK), jnp.float32)
            acc = jnp.zeros((rows, HD), jnp.float32)
            for s in range(LIST):
                powers = jnp.exp2((score_sc[chain, s] - row_max) * exp2_scale)
                total = total + powers
                value = v_ref[0, slot_ref[local, s], :, kv_lanes]
                acc = acc + jnp.dot(
                    powers.astype(jnp.bfloat16), value, preferred_element_type=jnp.float32
                )
            denominator = jnp.sum(total, axis=1, keepdims=True)
            result = (acc / denominator).astype(jnp.bfloat16)
            for k, j in enumerate(heads):
                o_ref[:, j * HD:(j + 1) * HD] = result[k * BLK:(k + 1) * BLK]
            chain += 1


def attend(slots, diag, queries, kv_buffer):
    blocks_here = queries.shape[0] // BLK
    buffer_blocks = kv_buffer.shape[1]
    flops = 4 * blocks_here * H * BLK * LIST * BLK * HD
    grid_spec = pltpu.PrefetchScalarGridSpec(
        num_scalar_prefetch=2,
        grid=(KVH // KV_STEP, blocks_here),
        in_specs=[
            pl.BlockSpec((BLK, KV_STEP * GROUP * HD), lambda g, b, *_: (b, g)),
            pl.BlockSpec((1, buffer_blocks, BLK, KV_STEP * HD), lambda g, b, *_: (0, 0, 0, g)),
            pl.BlockSpec((1, buffer_blocks, BLK, KV_STEP * HD), lambda g, b, *_: (1, 0, 0, g)),
        ],
        out_specs=pl.BlockSpec((BLK, KV_STEP * GROUP * HD), lambda g, b, *_: (b, g)),
        scratch_shapes=[
            pltpu.VMEM((KV_STEP * GROUP // PAIR, LIST, PAIR * BLK, BLK), jnp.float32),
            pltpu.VMEM((2, PAIR * BLK, BLK), jnp.float32),
        ],
    )
    return pl.pallas_call(
        attend_kernel,
        out_shape=jax.ShapeDtypeStruct(queries.shape, jnp.bfloat16),
        grid_spec=grid_spec,
        compiler_params=pltpu.CompilerParams(
            dimension_semantics=("arbitrary", "arbitrary"),
            vmem_limit_bytes=40 * 1024 * 1024,
        ),
        cost_estimate=pl.CostEstimate(
            flops=flops,
            transcendentals=blocks_here * H * BLK * LIST * BLK,
            bytes_accessed=2 * queries.size * 2 + kv_buffer.size * 2,
        ),
    )(slots, diag, queries, kv_buffer, kv_buffer)


def per_device(queries, key_rows, value_rows, pattern):
    tok_rows = queries.shape[0]
    blocks_here = tok_rows // BLK
    ctx_count = lax.axis_size("ctx")
    own_index = lax.axis_index("ctx")
    kv = jnp.stack([key_rows, value_rows])
    assert blocks_here == 2 and ctx_count % 4 == 0
    early = window_blocks(kv, "ctx")
    columns = blocks_here * ctx_count // STRIDE
    spread = STRIDE // blocks_here
    column_blocks = [
        tree_broadcast(kv[:, :BLK], "ctx", column * spread, ctx_count)
        for column in range(columns)
    ]
    buffer_blocks = columns + 4 * blocks_here + blocks_here
    kv_buffer = jnp.concatenate(column_blocks + early + [kv], axis=1).reshape(
        2, buffer_blocks, BLK, kv.shape[2]
    )
    first_block = own_index * blocks_here - 4 * blocks_here
    rows_pattern = lax.dynamic_slice_in_dim(pattern, own_index * blocks_here, blocks_here, 0)
    slots = jnp.where(
        rows_pattern >= first_block,
        columns + rows_pattern - first_block,
        rows_pattern // STRIDE,
    )
    slots = jnp.clip(slots, 0, buffer_blocks - 1).astype(jnp.int32)
    blocks = own_index * blocks_here + jnp.arange(blocks_here, dtype=jnp.int32)
    diag = (rows_pattern == blocks[:, None]).astype(jnp.int32)
    return attend(slots, diag, queries, kv_buffer)


def solution(mesh):
    placed = (
        P(("groups", "ctx"), None),
        P(("groups", "ctx"), None),
        P(("groups", "ctx"), None),
        P(),
    )
    return jax.shard_map(
        per_device,
        mesh=mesh,
        in_specs=placed,
        out_specs=P(("groups", "ctx"), None),
        check_vma=False,
    )
```

```python
import functools

import jax
import jax.numpy as jnp
from jax import lax
from jax.experimental import pallas as pl
from jax.experimental.pallas import tpu as pltpu
from jax.sharding import PartitionSpec as P

H = 32
KVH = 8
HD = 128
BLK = 128
WIN = 8
STRIDE = 32
LIST = 11
GROUP = H // KVH
PAIR = 2
KV_STEP = 4


def shifted(shard, axis, by, sends):
    size = lax.axis_size(axis)
    pairs = [(i, i + by) for i in range(size) if sends(i) and 0 <= i + by < size]
    return lax.ppermute(shard, axis, pairs)


def window_blocks(kv, axis):
    index = lax.axis_index(axis)
    y_low = (index // 2) % 2 == 0
    core0 = index % 2 == 0
    back4 = shifted(kv, axis, 4, lambda i: True)
    up_y = shifted(kv, axis, 2, lambda i: (i // 2) % 2 == 0)
    next_core = shifted(kv, axis, 1, lambda i: i % 2 == 0)
    down_y = shifted(back4, axis, -2, lambda i: (i // 2) % 2 == 1)
    back2 = jnp.where(y_low, down_y, up_y)
    partner_back4 = shifted(back4, axis, -1, lambda i: i % 2 == 1)
    size = lax.axis_size(axis)
    swap_pairs = [(i, i ^ 1) for i in range(size)]
    partner_back2 = lax.ppermute(back2, axis, swap_pairs)
    back3 = jnp.where(core0, partner_back4, partner_back2)
    back1 = jnp.where(core0, partner_back2, next_core)
    return [back4, back3, back2, back1]


def tree_broadcast(block, axis, source, size):
    index = lax.axis_index(axis)
    span = size - source
    held = block
    dist = 1
    while dist < span:
        dist *= 2
    dist //= 2
    while dist >= 1:
        pairs = [
            (source + j, source + j + dist)
            for j in range(0, span, 2 * dist)
            if j + dist < span
        ]
        got = lax.ppermute(held, axis, pairs)
        rel = index - source
        takes = (rel >= 0) & (rel % (2 * dist) == dist)
        held = jnp.where(takes, got, held)
        dist //= 2
    return held


def attend_kernel(slot_ref, diag_ref, q_ref, kv_ref, o_ref, score_sc, bias_sc):
    local = pl.program_id(1)
    base = pl.program_id(0) * KV_STEP * HD
    exp2_scale = (HD ** (-0.5)) * 1.4426950408889634
    rows = PAIR * BLK
    row = lax.broadcasted_iota(jnp.int32, (rows, BLK), 0) % BLK
    col = lax.broadcasted_iota(jnp.int32, (rows, BLK), 1)
    bias_sc[0] = jnp.zeros((rows, BLK), jnp.float32)
    bias_sc[1] = jnp.where(col > row, -jnp.inf, 0.0).astype(jnp.float32)
    q = q_ref[...]
    chain = 0
    for kv_head in range(KV_STEP):
        kv_lanes = pl.ds(pl.multiple_of(base + kv_head * HD, HD), HD)
        for half in range(GROUP // PAIR):
            heads = [kv_head * GROUP + j for j in range(half * PAIR, (half + 1) * PAIR)]
            stacked = jnp.concatenate([q[:, j * HD:(j + 1) * HD] for j in heads], axis=0)
            run_max = jnp.full((rows, BLK), -jnp.inf, jnp.float32)
            for s in range(LIST):
                key = kv_ref[0, slot_ref[local, s], :, kv_lanes]
                sc = lax.dot_general(
                    stacked, key, (((1,), (1,)), ((), ())), preferred_element_type=jnp.float32
                ) + bias_sc[diag_ref[local, s]]
                score_sc[chain, s] = sc
                run_max = jnp.maximum(run_max, sc)
            row_max = jnp.max(run_max, axis=1, keepdims=True)
            total = jnp.zeros((rows, BLK), jnp.float32)
            acc = jnp.zeros((rows, HD), jnp.float32)
            for s in range(LIST):
                powers = jnp.exp2((score_sc[chain, s] - row_max) * exp2_scale)
                total = total + powers
                value = kv_ref[1, slot_ref[local, s], :, kv_lanes]
                acc = acc + jnp.dot(
                    powers.astype(jnp.bfloat16), value, preferred_element_type=jnp.float32
                )
            denominator = jnp.sum(total, axis=1, keepdims=True)
            result = (acc / denominator).astype(jnp.bfloat16)
            for k, j in enumerate(heads):
                o_ref[:, j * HD:(j + 1) * HD] = result[k * BLK:(k + 1) * BLK]
            chain += 1


def attend(slots, diag, queries, kv_buffer):
    blocks_here = queries.shape[0] // BLK
    buffer_blocks = kv_buffer.shape[1]
    flops = 4 * blocks_here * H * BLK * LIST * BLK * HD
    grid_spec = pltpu.PrefetchScalarGridSpec(
        num_scalar_prefetch=2,
        grid=(KVH // KV_STEP, blocks_here),
        in_specs=[
            pl.BlockSpec((BLK, KV_STEP * GROUP * HD), lambda g, b, *_: (b, g)),
            pl.BlockSpec(memory_space=pltpu.VMEM),
        ],
        out_specs=pl.BlockSpec((BLK, KV_STEP * GROUP * HD), lambda g, b, *_: (b, g)),
        scratch_shapes=[
            pltpu.VMEM((KV_STEP * GROUP // PAIR, LIST, PAIR * BLK, BLK), jnp.float32),
            pltpu.VMEM((2, PAIR * BLK, BLK), jnp.float32),
        ],
    )
    return pl.pallas_call(
        attend_kernel,
        out_shape=jax.ShapeDtypeStruct(queries.shape, jnp.bfloat16),
        grid_spec=grid_spec,
        compiler_params=pltpu.CompilerParams(
            dimension_semantics=("arbitrary", "arbitrary"),
            vmem_limit_bytes=40 * 1024 * 1024,
        ),
        cost_estimate=pl.CostEstimate(
            flops=flops,
            transcendentals=blocks_here * H * BLK * LIST * BLK,
            bytes_accessed=2 * queries.size * 2 + kv_buffer.size * 2,
        ),
    )(slots, diag, queries, kv_buffer)


def per_device(queries, key_rows, value_rows, pattern):
    tok_rows = queries.shape[0]
    blocks_here = tok_rows // BLK
    ctx_count = lax.axis_size("ctx")
    own_index = lax.axis_index("ctx")
    kv = jnp.stack([key_rows, value_rows])
    assert blocks_here == 2 and ctx_count % 4 == 0
    early = window_blocks(kv, "ctx")
    columns = blocks_here * ctx_count // STRIDE
    spread = STRIDE // blocks_here
    column_blocks = [
        tree_broadcast(kv[:, :BLK], "ctx", column * spread, ctx_count)
        for column in range(columns)
    ]
    buffer_blocks = columns + 4 * blocks_here + blocks_here
    kv_buffer = jnp.concatenate(column_blocks + early + [kv], axis=1).reshape(
        2, buffer_blocks, BLK, kv.shape[2]
    )
    first_block = own_index * blocks_here - 4 * blocks_here
    rows_pattern = lax.dynamic_slice_in_dim(pattern, own_index * blocks_here, blocks_here, 0)
    slots = jnp.where(
        rows_pattern >= first_block,
        columns + rows_pattern - first_block,
        rows_pattern // STRIDE,
    )
    slots = jnp.clip(slots, 0, buffer_blocks - 1).astype(jnp.int32)
    blocks = own_index * blocks_here + jnp.arange(blocks_here, dtype=jnp.int32)
    diag = (rows_pattern == blocks[:, None]).astype(jnp.int32)
    return attend(slots, diag, queries, kv_buffer)


def solution(mesh):
    placed = (
        P(("groups", "ctx"), None),
        P(("groups", "ctx"), None),
        P(("groups", "ctx"), None),
        P(),
    )
    return jax.shard_map(
        per_device,
        mesh=mesh,
        in_specs=placed,
        out_specs=P(("groups", "ctx"), None),
        check_vma=False,
    )
```
